32 devices in a mesh: group: 16 (over z, x, core), slab: 2 (over y).
Axes of the slice: x: 2, y: 2, z: 4, core: 2. Of those that a mesh axis runs over, the one named last changes fastest.
Arguments:
- tokens: bfloat16 [16, 1024, 1024], P('group', 'slab'), may hold values from -6 to 6
- norm_gain: float32 [1024], replicated, may hold values from 0.1 to 1.9
- w_qkv: bfloat16 [1024, 3, 1024], P(None, None, 'slab'), may hold values from -0.1875 to 0.1875
- q_gain: float32 [64], replicated, may hold values from 0.5 to 3
- k_gain: float32 [64], replicated, may hold values from 0.5 to 3
- w_out: bfloat16 [1024, 1024], P('slab'), may hold values from -0.1875 to 0.1875
- covis_mask: int32 [16, 16], replicated, may hold values from 0 to 1, as said below
- capture_rank: int32 [16], replicated, may hold values from 0 to 15, each once
Outputs:
- mixed_rows: bfloat16 [16, 1024, 1024], P('group', 'slab')
The draws below stay inside these ranges and needn't reach their ends.
Inputs may be any that keep to these rules, and one draw needn't show every extreme that they name: covis_mask[i, j] is 1 where i = j, 0 where |i - j| > 3, and covis_mask[i, j] = covis_mask[j, i]. `capture_rank`: a permutation of the image numbers.
All inputs are finite; a program needn't handle non-finite values.
Results may differ from the reference program's by a relative error of at most 0.015.
The reference program's roundings to bfloat16 on the way (of `normed`, `weights` and `attended`) count: a program that leaves them out, or rounds other values in their place, can miss the bound.
Values may be sent and summed in bfloat16 or wider, within the bound.
No kernel may reach another device: no remote copies, remote signals or barrier semaphores. Data moves between devices by JAX's collectives and lax.ppermute only.
A program may use at most 64 MiB of HBM per device.

```python
import math
import jax
import jax.numpy as jnp
from jax import lax

D = 1024
HEADS = 16
HD = 64
TOK_IMG = 1024
REACH = 3
IMAGES = 16


def draw_covis_mask(key, part):
    coin_flip = jax.random.randint(key, (IMAGES, IMAGES), 0, 5)
    row_index = lax.broadcasted_iota(jnp.int32, (IMAGES, IMAGES), 0)
    col_index = lax.broadcasted_iota(jnp.int32, (IMAGES, IMAGES), 1)
    mirrored = jnp.where(row_index < col_index, coin_flip, jnp.transpose(coin_flip))
    in_band = jnp.abs(row_index - col_index) <= REACH
    linked = (mirrored < 3) & in_band | (row_index == col_index)
    return linked.astype(jnp.int32)


def steps_of(own_key, extent, cuts, least, largest):
    factor_of, own = 1.0, jax.random.fold_in(own_key, 6)
    for position, parts in cuts:
        heights = jnp.exp(jax.random.uniform(jax.random.fold_in(own, position), (parts,), jnp.float32, least / len(cuts), largest / len(cuts)))
        factor_of = factor_of * jnp.repeat(heights, extent[position] // parts).reshape([-1 if axis == position else 1 for axis in range(len(extent))])
    return factor_of


def bell_draw(stream_key, shape, scale, most, cuts=(), kind=jnp.bfloat16):
    result = jax.random.normal(stream_key, shape, jnp.float32) * scale
    if len(cuts) > 0:
        result = steps_of(stream_key, shape, cuts, -0.22, 0.18) * result
    return jnp.clip(result, min=-most, max=most).astype(kind)


def setup_inputs(seed: int = 0) -> dict:
    seeds = jax.random.split(jax.random.key(seed), 9)
    return {
        "tokens": bell_draw(seeds[0], (IMAGES, TOK_IMG, D), 1.0, 6.0, ((0, 16), (1, 2))),
        "norm_gain": jnp.clip(1.0 + 0.18 * jax.random.normal(seeds[1], (D,), jnp.float32), 0.1, 1.9),
        "w_qkv": bell_draw(seeds[2], (D, 3, D), D ** -0.5, 0.1875, ((2, 2),)),
        "q_gain": jnp.clip(jnp.exp(jax.random.uniform(seeds[3], (HD,), jnp.float32, math.log(0.5), math.log(3.0))), 0.5, 3.0),
        "k_gain": jnp.clip(jnp.exp(jax.random.uniform(seeds[4], (HD,), jnp.float32, math.log(0.5), math.log(3.0))), 0.5, 3.0),
        "w_out": bell_draw(seeds[5], (D, D), D ** -0.5, 0.1875, ((0, 2),)),
        "covis_mask": draw_covis_mask(jax.random.fold_in(seeds[8], 71), 0),
        "capture_rank": jax.random.permutation(seeds[7], IMAGES).astype(jnp.int32),
    }


def norm_rows(values, gain):
    centre = lax.optimization_barrier(jnp.mean(values, axis=-1, keepdims=True))
    centred = values - centre
    spread = lax.optimization_barrier(jnp.mean(centred * centred, axis=-1, keepdims=True))
    return centred * lax.rsqrt(spread + 1e-06) * gain

def block_terms(queries, key_rows, values):
    score_scale = HD ** (-0.5)
    scores = jnp.einsum('qhd,khd->hqk', queries.astype(jnp.float32), key_rows.astype(jnp.float32)) * score_scale
    weights = jnp.exp(scores).astype(jnp.bfloat16)
    numerator = jnp.einsum('hqk,khd->qhd', weights.astype(jnp.float32), values.astype(jnp.float32))
    denominator = jnp.transpose(lax.optimization_barrier(jnp.sum(weights.astype(jnp.float32), axis=2)))
    return (numerator, denominator)

def reference(tokens, norm_gain, w_qkv, q_gain, k_gain, w_out, covis_mask, capture_rank):
    flat_w = w_qkv.reshape(D, 3 * D)

    def split_heads(image):
        normed = norm_rows(image.astype(jnp.float32), norm_gain.astype(jnp.float32)).astype(jnp.bfloat16)
        projected = jnp.dot(normed, flat_w, preferred_element_type=jnp.float32).reshape(TOK_IMG, 3, HEADS, HD)
        queries = norm_rows(projected[:, 0], q_gain.astype(jnp.float32)).astype(jnp.bfloat16)
        key_rows = norm_rows(projected[:, 1], k_gain.astype(jnp.float32)).astype(jnp.bfloat16)
        values = projected[:, 2].astype(jnp.bfloat16)
        return (queries, key_rows, values)
    all_queries, all_keys, all_values = lax.map(split_heads, tokens)

    def attend(image_index):
        queries = all_queries[image_index]
        numerator = jnp.zeros((TOK_IMG, HEADS, HD), jnp.float32)
        denominator = jnp.zeros((TOK_IMG, HEADS), jnp.float32)
        for offset in range(-REACH, REACH + 1):
            partner = image_index + offset
            in_range = (partner >= 0) & (partner < IMAGES)
            clipped = jnp.clip(partner, 0, IMAGES - 1).astype(jnp.int32)
            allowed = in_range & (covis_mask[image_index, clipped] == 1) & (capture_rank[clipped] <= capture_rank[image_index])
            key_rows = all_keys[clipped]
            values = all_values[clipped]

            def taken():
                return block_terms(queries, key_rows, values)

            def skipped():
                return (jnp.zeros((TOK_IMG, HEADS, HD), jnp.float32), jnp.zeros((TOK_IMG, HEADS), jnp.float32))
            part_num, part_den = lax.cond(allowed, taken, skipped)
            numerator = numerator + part_num
            denominator = denominator + part_den
        attended = (numerator / denominator[:, :, None]).astype(jnp.bfloat16).reshape(TOK_IMG, D)
        return jnp.dot(attended, w_out, preferred_element_type=jnp.float32).astype(jnp.bfloat16)
    return lax.map(attend, jnp.arange(IMAGES, dtype=jnp.int32))
```

```python
import jax
import jax.numpy as jnp
from jax import lax
from jax.sharding import PartitionSpec as P

REACH = 3


def shifted(block, axis, distance):
    devices = range(lax.axis_size(axis))
    route = [(i - distance, i) for i in devices if i - distance in devices]
    return lax.ppermute(block, axis, route)


def rotated(block, axis, distance):
    count = lax.axis_size(axis)
    route = [(i, (i + distance) % count) for i in range(count)]
    return lax.ppermute(block, axis, route)


def norm_rows(values, gain):
    centre = jnp.mean(values, axis=-1, keepdims=True)
    centred = values - centre
    spread = jnp.mean(centred * centred, axis=-1, keepdims=True)
    return centred * lax.rsqrt(spread + 1e-06) * gain


def block_terms(queries, key_rows, values, score_scale):
    scores = (
        jnp.einsum("qhd,khd->hqk", queries, key_rows, preferred_element_type=jnp.float32)
        * score_scale
    )
    weights = jnp.exp(scores).astype(jnp.bfloat16)
    numerator = jnp.einsum("hqk,khd->qhd", weights, values, preferred_element_type=jnp.float32)
    denominator = jnp.transpose(jnp.sum(weights, axis=2, dtype=jnp.float32))
    return (numerator, denominator)


def body(tokens, norm_gain, w_qkv, q_gain, k_gain, w_out, covis_mask, capture_rank):
    full_width = tokens.shape[2]
    local_width = w_qkv.shape[2]
    head_size = q_gain.shape[0]
    heads_here = local_width // head_size
    score_scale = head_size ** (-0.5)
    slab_count = lax.axis_size("slab")
    normed = norm_rows(tokens[0].astype(jnp.float32), norm_gain).astype(jnp.bfloat16)
    piece_rows = normed.shape[0]
    flat_w = w_qkv.reshape(full_width, 3 * local_width)

    pieces = [normed] + [rotated(normed, "slab", k) for k in range(1, slab_count)]
    projected = jnp.concatenate(
        [jnp.dot(piece, flat_w, preferred_element_type=jnp.float32) for piece in pieces], axis=0
    )
    token_count = projected.shape[0]
    projected = projected.reshape(token_count, 3, heads_here, head_size)
    queries = norm_rows(projected[:, 0], q_gain).astype(jnp.bfloat16)
    key_rows = norm_rows(projected[:, 1], k_gain).astype(jnp.bfloat16)
    values = projected[:, 2].astype(jnp.bfloat16)
    my_group = lax.axis_index("group")
    group_count = lax.axis_size("group")

    def terms_from(source, keys_in, values_in):
        in_range = (source >= 0) & (source < group_count)
        clipped = jnp.clip(source, 0, group_count - 1)
        allowed = (
            in_range
            & (covis_mask[my_group, clipped] == 1)
            & (capture_rank[clipped] <= capture_rank[my_group])
        )

        def taken():
            return block_terms(queries, keys_in, values_in, score_scale)

        def skipped():
            return (
                jnp.zeros((token_count, heads_here, head_size), jnp.float32),
                jnp.zeros((token_count, heads_here), jnp.float32),
            )

        return lax.cond(allowed, taken, skipped)

    arrivals = []
    for hop_count in range(1, REACH + 1):
        arrivals.append((my_group - hop_count, shifted((key_rows, values), "group", hop_count)))
        arrivals.append((my_group + hop_count, shifted((key_rows, values), "group", -hop_count)))

    numerator, denominator = block_terms(queries, key_rows, values, score_scale)
    for source, (keys_in, values_in) in arrivals:
        part_num, part_den = terms_from(source, keys_in, values_in)
        numerator = numerator + part_num
        denominator = denominator + part_den
    attended = (
        (numerator / denominator[:, :, None]).astype(jnp.bfloat16).reshape(token_count, local_width)
    )

    mixed = None
    for k in range(slab_count - 1, -1, -1):
        chunk = jnp.dot(
            attended[k * piece_rows:(k + 1) * piece_rows], w_out, preferred_element_type=jnp.float32
        )
        if k == 0:
            mixed = chunk if mixed is None else mixed + chunk
        else:
            arrived = rotated(chunk.astype(jnp.bfloat16), "slab", -k).astype(jnp.float32)
            mixed = arrived if mixed is None else mixed + arrived
    return mixed.astype(jnp.bfloat16)[None]


def solution(mesh):
    placed = (
        P("group", "slab", None),
        P(),
        P(None, None, "slab"),
        P(),
        P(),
        P("slab", None),
        P(),
        P(),
    )
    return jax.shard_map(
        body, mesh=mesh, in_specs=placed, out_specs=P("group", "slab", None), check_vma=False
    )
```

```python
import jax
import jax.numpy as jnp
from jax import lax
from jax.sharding import PartitionSpec as P

REACH = 3


def shifted(block, axis, distance):
    devices = range(lax.axis_size(axis))
    route = [(i - distance, i) for i in devices if i - distance in devices]
    return lax.ppermute(block, axis, route)


def rotated(block, axis, distance):
    count = lax.axis_size(axis)
    route = [(i, (i + distance) % count) for i in range(count)]
    return lax.ppermute(block, axis, route)


def norm_rows(values, gain):
    centre = jnp.mean(values, axis=-1, keepdims=True)
    centred = values - centre
    spread = jnp.mean(centred * centred, axis=-1, keepdims=True)
    return centred * lax.rsqrt(spread + 1e-06) * gain


def block_terms(queries, key_rows, values, score_scale):
    scores = (
        jnp.einsum("qhd,khd->hqk", queries, key_rows, preferred_element_type=jnp.float32)
        * score_scale
    )
    weights = jnp.exp(scores).astype(jnp.bfloat16)
    numerator = jnp.einsum("hqk,khd->qhd", weights, values, preferred_element_type=jnp.float32)
    denominator = jnp.transpose(jnp.sum(weights, axis=2, dtype=jnp.float32))
    return (numerator, denominator)


def set_terms(queries, key_sets, score_scale):
    numerator, denominator = None, None
    for key_rows, values in key_sets:
        part_num, part_den = block_terms(queries, key_rows, values, score_scale)
        if numerator is None:
            numerator, denominator = part_num, part_den
        else:
            numerator, denominator = numerator + part_num, denominator + part_den
    return numerator, denominator


def body(tokens, norm_gain, w_qkv, q_gain, k_gain, w_out, covis_mask, capture_rank):
    full_width = tokens.shape[2]
    local_width = w_qkv.shape[2]
    head_size = q_gain.shape[0]
    heads_here = local_width // head_size
    score_scale = head_size ** (-0.5)
    slab_count = lax.axis_size("slab")
    my_group = lax.axis_index("group")
    group_count = lax.axis_size("group")
    normed = norm_rows(tokens[0].astype(jnp.float32), norm_gain).astype(jnp.bfloat16)
    piece_rows = normed.shape[0]
    flat_w = w_qkv.reshape(full_width, 3 * local_width)

    def project(rows):
        projected = jnp.dot(rows, flat_w, preferred_element_type=jnp.float32)
        projected = projected.reshape(rows.shape[0], 3, heads_here, head_size)
        queries = norm_rows(projected[:, 0], q_gain).astype(jnp.bfloat16)
        key_rows = norm_rows(projected[:, 1], k_gain).astype(jnp.bfloat16)
        values = projected[:, 2].astype(jnp.bfloat16)
        return queries, key_rows, values

    own_q, own_k, own_v = project(normed)
    key_sets = [(own_k, own_v)]
    queries = own_q
    if slab_count > 1:
        others = jnp.concatenate(
            [rotated(normed, "slab", k) for k in range(1, slab_count)], axis=0
        )
        rest_q, rest_k, rest_v = project(others)
        key_sets.append((rest_k, rest_v))
        queries = jnp.concatenate([own_q, rest_q], axis=0)
    token_count = queries.shape[0]

    def allowed_from(source):
        in_range = (source >= 0) & (source < group_count)
        clipped = jnp.clip(source, 0, group_count - 1)
        return (
            in_range
            & (covis_mask[my_group, clipped] == 1)
            & (capture_rank[clipped] <= capture_rank[my_group])
        )

    def masked_terms(source, rows, sets):
        row_count = rows.stop - rows.start

        def taken():
            return set_terms(queries[rows], sets, score_scale)

        def skipped():
            return (
                jnp.zeros((row_count, heads_here, head_size), jnp.float32),
                jnp.zeros((row_count, heads_here), jnp.float32),
            )

        return lax.cond(allowed_from(source), taken, skipped)

    all_rows = slice(0, token_count)
    forward = [shifted(pair, "group", 1) for pair in key_sets]
    backward = [shifted(pair, "group", -1) for pair in key_sets]
    numerator, denominator = set_terms(queries, key_sets, score_scale)
    forward, backward, numerator, denominator = lax.optimization_barrier(
        (forward, backward, numerator, denominator)
    )
    for hop_count in range(2, REACH + 1):
        next_forward = [shifted(pair, "group", 1) for pair in forward]
        next_backward = [shifted(pair, "group", -1) for pair in backward]
        for source, sets in ((my_group - hop_count + 1, forward), (my_group + hop_count - 1, backward)):
            part_num, part_den = masked_terms(source, all_rows, sets)
            numerator, denominator = numerator + part_num, denominator + part_den
        forward, backward, numerator, denominator = lax.optimization_barrier(
            (next_forward, next_backward, numerator, denominator)
        )

    mixed = None
    for k in list(range(1, slab_count)) + [0]:
        rows = slice(k * piece_rows, (k + 1) * piece_rows)
        chunk_num, chunk_den = numerator[rows], denominator[rows]
        for source, sets in ((my_group - REACH, forward), (my_group + REACH, backward)):
            part_num, part_den = masked_terms(source, rows, sets)
            chunk_num, chunk_den = chunk_num + part_num, chunk_den + part_den
        attended = (
            (chunk_num / chunk_den[:, :, None]).astype(jnp.bfloat16).reshape(piece_rows, local_width)
        )
        chunk = jnp.dot(attended, w_out, preferred_element_type=jnp.float32)
        if k != 0:
            outgoing, forward, backward, numerator, denominator = lax.optimization_barrier(
                (chunk.astype(jnp.bfloat16), forward, backward, numerator, denominator)
            )
            chunk = rotated(outgoing, "slab", -k).astype(jnp.float32)
        mixed = chunk if mixed is None else mixed + chunk
    return mixed.astype(jnp.bfloat16)[None]


def solution(mesh):
    placed = (
        P("group", "slab", None),
        P(),
        P(None, None, "slab"),
        P(),
        P(),
        P("slab", None),
        P(),
        P(),
    )
    return jax.shard_map(
        body, mesh=mesh, in_specs=placed, out_specs=P("group", "slab", None), check_vma=False
    )
```

```python
import jax
import jax.numpy as jnp
from jax import lax
from jax.sharding import PartitionSpec as P

REACH = 3


def shifted(block, axis, distance):
    devices = range(lax.axis_size(axis))
    route = [(i - distance, i) for i in devices if i - distance in devices]
    return lax.ppermute(block, axis, route)


def rotated(block, axis, distance):
    count = lax.axis_size(axis)
    route = [(i, (i + distance) % count) for i in range(count)]
    return lax.ppermute(block, axis, route)


def norm_rows(values, gain):
    centre = jnp.mean(values, axis=-1, keepdims=True)
    centred = values - centre
    spread = jnp.mean(centred * centred, axis=-1, keepdims=True)
    return centred * lax.rsqrt(spread + 1e-06) * gain


def block_terms(queries, key_rows, values, score_scale):
    scores = (
        jnp.einsum("qhd,khd->hqk", queries, key_rows, preferred_element_type=jnp.float32)
        * score_scale
    )
    weights = jnp.exp(scores).astype(jnp.bfloat16)
    numerator = jnp.einsum("hqk,khd->qhd", weights, values, preferred_element_type=jnp.float32)
    denominator = jnp.transpose(jnp.sum(weights, axis=2, dtype=jnp.float32))
    return (numerator, denominator)


def set_terms(queries, key_sets, score_scale):
    numerator, denominator = None, None
    for key_rows, values in key_sets:
        part_num, part_den = block_terms(queries, key_rows, values, score_scale)
        if numerator is None:
            numerator, denominator = part_num, part_den
        else:
            numerator, denominator = numerator + part_num, denominator + part_den
    return numerator, denominator


def body(tokens, norm_gain, w_qkv, q_gain, k_gain, w_out, covis_mask, capture_rank):
    full_width = tokens.shape[2]
    local_width = w_qkv.shape[2]
    head_size = q_gain.shape[0]
    heads_here = local_width // head_size
    score_scale = head_size ** (-0.5)
    slab_count = lax.axis_size("slab")
    my_group = lax.axis_index("group")
    group_count = lax.axis_size("group")
    normed = norm_rows(tokens[0].astype(jnp.float32), norm_gain).astype(jnp.bfloat16)
    piece_rows = normed.shape[0]
    flat_w = w_qkv.reshape(full_width, 3 * local_width)

    def project(rows):
        projected = jnp.dot(rows, flat_w, preferred_element_type=jnp.float32)
        projected = projected.reshape(rows.shape[0], 3, heads_here, head_size)
        queries = norm_rows(projected[:, 0], q_gain).astype(jnp.bfloat16)
        key_rows = norm_rows(projected[:, 1], k_gain).astype(jnp.bfloat16)
        values = projected[:, 2].astype(jnp.bfloat16)
        return queries, jnp.stack([key_rows, values], axis=1)

    queries, pairs = project(normed)
    if slab_count > 1:
        others = jnp.concatenate(
            [rotated(normed, "slab", k) for k in range(1, slab_count)], axis=0
        )
        rest_q, rest_pairs = project(others)
        queries = jnp.concatenate([queries, rest_q], axis=0)
        pairs = jnp.concatenate([pairs, rest_pairs], axis=0)
    token_count = queries.shape[0]

    def allowed_from(source):
        in_range = (source >= 0) & (source < group_count)
        clipped = jnp.clip(source, 0, group_count - 1)
        return (
            in_range
            & (covis_mask[my_group, clipped] == 1)
            & (capture_rank[clipped] <= capture_rank[my_group])
        )

    def pair_terms(rows, held):
        return block_terms(queries[rows], held[:, 0], held[:, 1], score_scale)

    def masked_terms(source, rows, held):
        row_count = rows.stop - rows.start

        def skipped():
            return (
                jnp.zeros((row_count, heads_here, head_size), jnp.float32),
                jnp.zeros((row_count, heads_here), jnp.float32),
            )

        return lax.cond(allowed_from(source), lambda: pair_terms(rows, held), skipped)

    def routed(block, route):
        return lax.ppermute(block, "group", [(a, b) for a, b in route if 0 <= b < group_count])

    g_all = range(group_count)
    spot = my_group % 4
    low = spot < 2
    even = spot % 2 == 0
    on_chip = [(g, g ^ 1) for g in g_all]
    across_x = [(g, g ^ 2) for g in g_all]
    along_z_once = [(g, g + 3) if g % 2 == 1 else (g, g - 3) for g in g_all]
    along_z_relay = [(g, g + 4) if g % 4 < 2 else (g, g - 4) for g in g_all]

    all_rows = slice(0, token_count)
    round_one = [
        (my_group ^ 1, routed(pairs, on_chip)),
        (my_group ^ 2, routed(pairs, across_x)),
        (jnp.where(even, my_group - 3, my_group + 3), routed(pairs, along_z_once)),
    ]
    numerator, denominator = pair_terms(all_rows, pairs)
    round_one, numerator, denominator = lax.optimization_barrier((round_one, numerator, denominator))
    from_x = round_one[1][1]
    round_two = [
        (my_group ^ 3, routed(from_x, on_chip)),
        (jnp.where(low, my_group - 2, my_group + 2), routed(from_x, along_z_relay)),
    ]
    for source, held in round_one:
        part_num, part_den = masked_terms(source, all_rows, held)
        numerator, denominator = numerator + part_num, denominator + part_den
    round_two, numerator, denominator = lax.optimization_barrier((round_two, numerator, denominator))
    from_z = round_two[1][1]
    last_source = jnp.where(
        spot == 0, my_group - 1, jnp.where(spot == 1, my_group - 3, jnp.where(spot == 2, my_group + 3, my_group + 1))
    )
    last_held = routed(from_z, on_chip)
    for source, held in round_two:
        part_num, part_den = masked_terms(source, all_rows, held)
        numerator, denominator = numerator + part_num, denominator + part_den
    last_held, numerator, denominator = lax.optimization_barrier((last_held, numerator, denominator))

    mixed = None
    for k in list(range(1, slab_count)) + [0]:
        rows = slice(k * piece_rows, (k + 1) * piece_rows)
        part_num, part_den = masked_terms(last_source, rows, last_held)
        chunk_num, chunk_den = numerator[rows] + part_num, denominator[rows] + part_den
        attended = (
            (chunk_num / chunk_den[:, :, None]).astype(jnp.bfloat16).reshape(piece_rows, local_width)
        )
        chunk = jnp.dot(attended, w_out, preferred_element_type=jnp.float32)
        if k != 0:
            outgoing, last_held, numerator, denominator = lax.optimization_barrier(
                (chunk.astype(jnp.bfloat16), last_held, numerator, denominator)
            )
            chunk = rotated(outgoing, "slab", -k).astype(jnp.float32)
        mixed = chunk if mixed is None else mixed + chunk
    return mixed.astype(jnp.bfloat16)[None]


def solution(mesh):
    placed = (
        P("group", "slab", None),
        P(),
        P(None, None, "slab"),
        P(),
        P(),
        P("slab", None),
        P(),
        P(),
    )
    return jax.shard_map(
        body, mesh=mesh, in_specs=placed, out_specs=P("group", "slab", None), check_vma=False
    )
```

```python
import functools

import jax
import jax.numpy as jnp
from jax import lax
from jax.sharding import PartitionSpec as P
from jax.experimental import pallas as pl
from jax.experimental.pallas import tpu as pltpu

REACH = 3


def shifted(block, axis, distance):
    devices = range(lax.axis_size(axis))
    route = [(i - distance, i) for i in devices if i - distance in devices]
    return lax.ppermute(block, axis, route)


def rotated(block, axis, distance):
    count = lax.axis_size(axis)
    route = [(i, (i + distance) % count) for i in range(count)]
    return lax.ppermute(block, axis, route)


def norm_rows(values, gain):
    centre = jnp.mean(values, axis=-1, keepdims=True)
    centred = values - centre
    spread = jnp.mean(centred * centred, axis=-1, keepdims=True)
    return centred * lax.rsqrt(spread + 1e-06) * gain


def block_terms(queries, key_rows, values, score_scale):
    scores = (
        jnp.einsum("qhd,khd->hqk", queries, key_rows, preferred_element_type=jnp.float32)
        * score_scale
    )
    weights = jnp.exp(scores).astype(jnp.bfloat16)
    numerator = jnp.einsum("hqk,khd->qhd", weights, values, preferred_element_type=jnp.float32)
    denominator = jnp.transpose(jnp.sum(weights, axis=2, dtype=jnp.float32))
    return (numerator, denominator)


def attention_kernel(q_ref, k_ref, v_ref, num_in, den_in, num_out, den_out, *, head_size, scale):
    queries = q_ref[...]
    keys = k_ref[...]
    values = v_ref[...]
    first = lax.broadcasted_iota(jnp.int32, (1, 2 * head_size), 1) < head_size
    parts = []
    for lanes in (first, jnp.logical_not(first)):
        head_keys = jnp.where(lanes, keys, jnp.zeros_like(keys))
        scores = lax.dot_general(
            queries, head_keys, (((1,), (1,)), ((), ())), preferred_element_type=jnp.float32
        ) * scale
        weights = jnp.exp(scores).astype(jnp.bfloat16)
        numerator = jnp.dot(weights, values, preferred_element_type=jnp.float32)
        denominator = jnp.sum(weights.astype(jnp.float32), axis=1, keepdims=True)
        parts.append((numerator, denominator))
    num_out[...] = num_in[...] + jnp.where(first, parts[0][0], parts[1][0])
    den_out[...] = den_in[...] + jnp.where(first, parts[0][1], parts[1][1])


def attend_block(queries, held, numerator, denominator, row_start, row_count, head_size, scale):
    token_count, width = queries.shape
    key_count = held.shape[1]
    pair_width = 2 * head_size
    tile = min(row_count, 512)
    first_tile = row_start // tile
    row_spec = pl.BlockSpec((tile, pair_width), lambda i, j: (i + first_tile, j))
    key_spec = pl.BlockSpec((None, key_count, pair_width), lambda i, j: (0, 0, j))
    value_spec = pl.BlockSpec((None, key_count, pair_width), lambda i, j: (1, 0, j))
    flops = 2 * 2 * 2 * row_count * key_count * width
    return pl.pallas_call(
        functools.partial(attention_kernel, head_size=head_size, scale=scale),
        grid=(row_count // tile, width // pair_width),
        in_specs=[row_spec, key_spec, value_spec, row_spec, row_spec],
        out_specs=[row_spec, row_spec],
        out_shape=[jax.ShapeDtypeStruct((token_count, width), jnp.float32)] * 2,
        input_output_aliases={3: 0, 4: 1},
        compiler_params=pltpu.CompilerParams(dimension_semantics=("arbitrary", "arbitrary")),
        cost_estimate=pl.CostEstimate(
            flops=flops,
            transcendentals=row_count * key_count * (width // head_size),
            bytes_accessed=row_count * width * 18 + key_count * width * 4 * (row_count // tile),
        ),
    )(queries, held, held, numerator, denominator)


def body(tokens, norm_gain, w_qkv, q_gain, k_gain, w_out, covis_mask, capture_rank):
    full_width = tokens.shape[2]
    local_width = w_qkv.shape[2]
    head_size = q_gain.shape[0]
    heads_here = local_width // head_size
    score_scale = head_size ** (-0.5)
    slab_count = lax.axis_size("slab")
    my_group = lax.axis_index("group")
    group_count = lax.axis_size("group")
    normed = norm_rows(tokens[0].astype(jnp.float32), norm_gain).astype(jnp.bfloat16)
    piece_rows = normed.shape[0]
    flat_w = w_qkv.reshape(full_width, 3 * local_width)

    def project(rows):
        projected = jnp.dot(rows, flat_w, preferred_element_type=jnp.float32)
        projected = projected.reshape(rows.shape[0], 3, heads_here, head_size)
        queries = norm_rows(projected[:, 0], q_gain).astype(jnp.bfloat16)
        key_rows = norm_rows(projected[:, 1], k_gain).astype(jnp.bfloat16)
        values = projected[:, 2].astype(jnp.bfloat16)
        flat = (rows.shape[0], local_width)
        return queries.reshape(flat), jnp.stack([key_rows.reshape(flat), values.reshape(flat)])

    queries, pairs = project(normed)
    if slab_count > 1:
        others = jnp.concatenate(
            [rotated(normed, "slab", k) for k in range(1, slab_count)], axis=0
        )
        rest_q, rest_pairs = project(others)
        queries = jnp.concatenate([queries, rest_q], axis=0)
        pairs = jnp.concatenate([pairs, rest_pairs], axis=1)
    token_count = queries.shape[0]

    def allowed_from(source):
        in_range = (source >= 0) & (source < group_count)
        clipped = jnp.clip(source, 0, group_count - 1)
        return (
            in_range
            & (covis_mask[my_group, clipped] == 1)
            & (capture_rank[clipped] <= capture_rank[my_group])
        )

    def add_terms(held, sums, row_start=0, row_count=None):
        row_count = token_count if row_count is None else row_count
        return tuple(
            attend_block(queries, held, sums[0], sums[1], row_start, row_count, head_size, score_scale)
        )

    def add_masked(source, held, sums, row_start=0, row_count=None):
        return lax.cond(
            allowed_from(source),
            lambda: add_terms(held, sums, row_start, row_count),
            lambda: sums,
        )

    def routed(block, route):
        return lax.ppermute(block, "group", [(a, b) for a, b in route if 0 <= b < group_count])

    g_all = range(group_count)
    spot = my_group % 4
    low = spot < 2
    even = spot % 2 == 0
    on_chip = [(g, g ^ 1) for g in g_all]
    across_x = [(g, g ^ 2) for g in g_all]
    along_z_once = [(g, g + 3) if g % 2 == 1 else (g, g - 3) for g in g_all]
    along_z_relay = [(g, g + 4) if g % 4 < 2 else (g, g - 4) for g in g_all]

    round_one = [
        (my_group ^ 1, routed(pairs, on_chip)),
        (my_group ^ 2, routed(pairs, across_x)),
        (jnp.where(even, my_group - 3, my_group + 3), routed(pairs, along_z_once)),
    ]
    zeros = jnp.zeros((token_count, local_width), jnp.float32)
    sums = add_terms(pairs, (zeros, zeros))
    round_one, sums = lax.optimization_barrier((round_one, sums))
    from_x = round_one[1][1]
    round_two = [
        (my_group ^ 3, routed(from_x, on_chip)),
        (jnp.where(low, my_group - 2, my_group + 2), routed(from_x, along_z_relay)),
    ]
    for source, held in round_one:
        sums = add_masked(source, held, sums)
    round_two, sums = lax.optimization_barrier((round_two, sums))
    from_z = round_two[1][1]
    last_source = jnp.where(
        spot == 0, my_group - 1, jnp.where(spot == 1, my_group - 3, jnp.where(spot == 2, my_group + 3, my_group + 1))
    )
    last_held = routed(from_z, on_chip)
    for source, held in round_two:
        sums = add_masked(source, held, sums)
    last_held, sums = lax.optimization_barrier((last_held, sums))

    mixed = None
    for k in list(range(1, slab_count)) + [0]:
        row_start = k * piece_rows
        sums = add_masked(last_source, last_held, sums, row_start, piece_rows)
        rows = slice(row_start, row_start + piece_rows)
        attended = (sums[0][rows] / sums[1][rows]).astype(jnp.bfloat16)
        chunk = jnp.dot(attended, w_out, preferred_element_type=jnp.float32)
        if k != 0:
            outgoing, last_held, sums = lax.optimization_barrier(
                (chunk.astype(jnp.bfloat16), last_held, sums)
            )
            chunk = rotated(outgoing, "slab", -k).astype(jnp.float32)
        mixed = chunk if mixed is None else mixed + chunk
    return mixed.astype(jnp.bfloat16)[None]


def solution(mesh):
    placed = (
        P("group", "slab", None),
        P(),
        P(None, None, "slab"),
        P(),
        P(),
        P("slab", None),
        P(),
        P(),
    )
    return jax.shard_map(
        body, mesh=mesh, in_specs=placed, out_specs=P("group", "slab", None), check_vma=False
    )
```

```python
import functools

import jax
import jax.numpy as jnp
from jax import lax
from jax.sharding import PartitionSpec as P
from jax.experimental import pallas as pl
from jax.experimental.pallas import tpu as pltpu

REACH = 3


def shifted(block, axis, distance):
    devices = range(lax.axis_size(axis))
    route = [(i - distance, i) for i in devices if i - distance in devices]
    return lax.ppermute(block, axis, route)


def rotated(block, axis, distance):
    count = lax.axis_size(axis)
    route = [(i, (i + distance) % count) for i in range(count)]
    return lax.ppermute(block, axis, route)


def norm_rows(values, gain):
    centre = jnp.mean(values, axis=-1, keepdims=True)
    centred = values - centre
    spread = jnp.mean(centred * centred, axis=-1, keepdims=True)
    return centred * lax.rsqrt(spread + 1e-06) * gain


def block_terms(queries, key_rows, values, score_scale):
    scores = (
        jnp.einsum("qhd,khd->hqk", queries, key_rows, preferred_element_type=jnp.float32)
        * score_scale
    )
    weights = jnp.exp(scores).astype(jnp.bfloat16)
    numerator = jnp.einsum("hqk,khd->qhd", weights, values, preferred_element_type=jnp.float32)
    denominator = jnp.transpose(jnp.sum(weights, axis=2, dtype=jnp.float32))
    return (numerator, denominator)


def attention_kernel(q_ref, k_ref, v_ref, num_in, den_in, num_out, den_out, *, head_size, scale):
    queries = q_ref[...]
    keys = k_ref[...]
    values = v_ref[...]
    first = lax.broadcasted_iota(jnp.int32, (1, 2 * head_size), 1) < head_size
    parts = []
    for lanes in (first, jnp.logical_not(first)):
        head_keys = jnp.where(lanes, keys, jnp.zeros_like(keys))
        scores = lax.dot_general(
            queries, head_keys, (((1,), (1,)), ((), ())), preferred_element_type=jnp.float32
        ) * scale
        weights = jnp.exp(scores).astype(jnp.bfloat16)
        numerator = jnp.dot(weights, values, preferred_element_type=jnp.float32)
        denominator = jnp.sum(weights.astype(jnp.float32), axis=1, keepdims=True)
        parts.append((numerator, denominator))
    num_out[...] = num_in[...] + jnp.where(first, parts[0][0], parts[1][0])
    den_out[...] = den_in[...] + jnp.where(first, parts[0][1], parts[1][1])


def attend_block(queries, held, numerator, denominator, row_start, row_count, head_size, scale):
    token_count, width = queries.shape
    key_count = held.shape[1]
    pair_width = 2 * head_size
    tile = min(row_count, 512)
    first_tile = row_start // tile
    row_spec = pl.BlockSpec((tile, pair_width), lambda i, j: (i + first_tile, j))
    key_spec = pl.BlockSpec((None, key_count, pair_width), lambda i, j: (0, 0, j))
    value_spec = pl.BlockSpec((None, key_count, pair_width), lambda i, j: (1, 0, j))
    flops = 2 * 2 * 2 * row_count * key_count * width
    return pl.pallas_call(
        functools.partial(attention_kernel, head_size=head_size, scale=scale),
        grid=(row_count // tile, width // pair_width),
        in_specs=[row_spec, key_spec, value_spec, row_spec, row_spec],
        out_specs=[row_spec, row_spec],
        out_shape=[jax.ShapeDtypeStruct((token_count, width), jnp.float32)] * 2,
        input_output_aliases={3: 0, 4: 1},
        compiler_params=pltpu.CompilerParams(dimension_semantics=("arbitrary", "arbitrary")),
        cost_estimate=pl.CostEstimate(
            flops=flops,
            transcendentals=row_count * key_count * (width // head_size),
            bytes_accessed=row_count * width * 18 + key_count * width * 4 * (row_count // tile),
        ),
    )(queries, held, held, numerator, denominator)


def body(tokens, norm_gain, w_qkv, q_gain, k_gain, w_out, covis_mask, capture_rank):
    full_width = tokens.shape[2]
    local_width = w_qkv.shape[2]
    head_size = q_gain.shape[0]
    heads_here = local_width // head_size
    score_scale = head_size ** (-0.5)
    slab_count = lax.axis_size("slab")
    my_group = lax.axis_index("group")
    group_count = lax.axis_size("group")
    normed = norm_rows(tokens[0].astype(jnp.float32), norm_gain).astype(jnp.bfloat16)
    piece_rows = normed.shape[0]
    flat_w = w_qkv.reshape(full_width, 3 * local_width)

    def project(rows):
        projected = jnp.dot(rows, flat_w, preferred_element_type=jnp.float32)
        projected = projected.reshape(rows.shape[0], 3, heads_here, head_size)
        queries = norm_rows(projected[:, 0], q_gain).astype(jnp.bfloat16)
        key_rows = norm_rows(projected[:, 1], k_gain).astype(jnp.bfloat16)
        values = projected[:, 2].astype(jnp.bfloat16)
        flat = (rows.shape[0], local_width)
        return queries.reshape(flat), jnp.stack([key_rows.reshape(flat), values.reshape(flat)])

    own_q, own_pairs = project(normed)

    def allowed_from(source):
        in_range = (source >= 0) & (source < group_count)
        clipped = jnp.clip(source, 0, group_count - 1)
        return (
            in_range
            & (covis_mask[my_group, clipped] == 1)
            & (capture_rank[clipped] <= capture_rank[my_group])
        )

    def routed(block, route):
        return lax.ppermute(block, "group", [(a, b) for a, b in route if 0 <= b < group_count])

    g_all = range(group_count)
    spot = my_group % 4
    on_chip = [(g, g ^ 1) for g in g_all]
    across_x = [(g, g ^ 2) for g in g_all]
    along_z_once = [(g, g + 3) if g % 2 == 1 else (g, g - 3) for g in g_all]
    along_z_relay = [(g, g + 4) if g % 4 < 2 else (g, g - 4) for g in g_all]

    def round_one(buf):
        return [
            (my_group ^ 1, routed(buf, on_chip)),
            (my_group ^ 2, routed(buf, across_x)),
            (jnp.where(spot % 2 == 0, my_group - 3, my_group + 3), routed(buf, along_z_once)),
        ]

    def round_two(first):
        from_x = first[1][1]
        return [
            (my_group ^ 3, routed(from_x, on_chip)),
            (jnp.where(spot < 2, my_group - 2, my_group + 2), routed(from_x, along_z_relay)),
        ]

    def round_three(second):
        source = jnp.where(
            spot == 0,
            my_group - 1,
            jnp.where(spot == 1, my_group - 3, jnp.where(spot == 2, my_group + 3, my_group + 1)),
        )
        return [(source, routed(second[1][1], on_chip))]

    own_first = round_one(own_pairs)
    queries, rest_pairs = own_q, None
    w_pieces = [w_out]
    if slab_count > 1:
        gathered = [rotated(normed, "slab", k) for k in range(1, slab_count)]
        w_later = lax.optimization_barrier((w_out, gathered))[0]
        w_pieces += [rotated(w_later, "slab", -k) for k in range(1, slab_count)]
        rest_q, rest_pairs = project(jnp.concatenate(gathered, axis=0))
        queries = jnp.concatenate([own_q, rest_q], axis=0)
    token_count = queries.shape[0]

    def add_terms(held, sums, row_start=0, row_count=None):
        row_count = token_count if row_count is None else row_count
        return tuple(
            attend_block(queries, held, sums[0], sums[1], row_start, row_count, head_size, score_scale)
        )

    def add_masked(arrived, sums, row_start=0, row_count=None):
        for source, held in arrived:
            sums = lax.cond(
                allowed_from(source),
                lambda: add_terms(held, sums, row_start, row_count),
                lambda: sums,
            )
        return sums

    zeros = jnp.zeros((token_count, local_width), jnp.float32)
    sums = add_terms(own_pairs, (zeros, zeros))
    if rest_pairs is None:
        own_first, sums = lax.optimization_barrier((own_first, sums))
        own_second = round_two(own_first)
        sums = add_masked(own_first, sums)
        own_second, sums = lax.optimization_barrier((own_second, sums))
        last = round_three(own_second)
        sums = add_masked(own_second, sums)
    else:
        rest_first = round_one(rest_pairs)
        sums = add_terms(rest_pairs, sums)
        own_first, sums = lax.optimization_barrier((own_first, sums))
        own_second = round_two(own_first)
        sums = add_masked(own_first, sums)
        own_second, rest_first, sums = lax.optimization_barrier((own_second, rest_first, sums))
        own_third = round_three(own_second)
        rest_second = round_two(rest_first)
        sums = add_masked(own_second + rest_first, sums)
        own_third, rest_second, sums = lax.optimization_barrier((own_third, rest_second, sums))
        last = round_three(rest_second)
        sums = add_masked(own_third + rest_second, sums)
    last, sums = lax.optimization_barrier((last, sums))

    att_pieces = [None] * slab_count
    for k in list(range(1, slab_count)) + [0]:
        row_start = k * piece_rows
        sums = add_masked(last, sums, row_start, piece_rows)
        rows = slice(row_start, row_start + piece_rows)
        attended = (sums[0][rows] / sums[1][rows]).astype(jnp.bfloat16)
        if k != 0:
            attended, last, sums = lax.optimization_barrier((attended, last, sums))
            attended = rotated(attended, "slab", -k)
        att_pieces[k] = attended
    mixed = jnp.dot(
        jnp.concatenate(att_pieces, axis=1),
        jnp.concatenate(w_pieces, axis=0),
        preferred_element_type=jnp.float32,
    )
    return mixed.astype(jnp.bfloat16)[None]


def solution(mesh):
    placed = (
        P("group", "slab", None),
        P(),
        P(None, None, "slab"),
        P(),
        P(),
        P("slab", None),
        P(),
        P(),
    )
    return jax.shard_map(
        body, mesh=mesh, in_specs=placed, out_specs=P("group", "slab", None), check_vma=False
    )
```

```python
import functools

import jax
import jax.numpy as jnp
from jax import lax
from jax.sharding import PartitionSpec as P
from jax.experimental import pallas as pl
from jax.experimental.pallas import tpu as pltpu

REACH = 3


def shifted(block, axis, distance):
    devices = range(lax.axis_size(axis))
    route = [(i - distance, i) for i in devices if i - distance in devices]
    return lax.ppermute(block, axis, route)


def rotated(block, axis, distance):
    count = lax.axis_size(axis)
    route = [(i, (i + distance) % count) for i in range(count)]
    return lax.ppermute(block, axis, route)


def norm_rows(values, gain):
    centre = jnp.mean(values, axis=-1, keepdims=True)
    centred = values - centre
    spread = jnp.mean(centred * centred, axis=-1, keepdims=True)
    return centred * lax.rsqrt(spread + 1e-06) * gain


def block_terms(queries, key_rows, values, score_scale):
    scores = (
        jnp.einsum("qhd,khd->hqk", queries, key_rows, preferred_element_type=jnp.float32)
        * score_scale
    )
    weights = jnp.exp(scores).astype(jnp.bfloat16)
    numerator = jnp.einsum("hqk,khd->qhd", weights, values, preferred_element_type=jnp.float32)
    denominator = jnp.transpose(jnp.sum(weights, axis=2, dtype=jnp.float32))
    return (numerator, denominator)


def attention_kernel(q_ref, k_ref, v_ref, num_in, den_in, num_out, den_out, *, head_size, scale):
    queries = q_ref[...]
    keys = k_ref[...]
    values = v_ref[...]
    first = lax.broadcasted_iota(jnp.int32, (1, 2 * head_size), 1) < head_size
    parts = []
    for lanes in (first, jnp.logical_not(first)):
        head_keys = jnp.where(lanes, keys, jnp.zeros_like(keys))
        scores = lax.dot_general(
            queries, head_keys, (((1,), (1,)), ((), ())), preferred_element_type=jnp.float32
        ) * scale
        weights = jnp.exp(scores).astype(jnp.bfloat16)
        numerator = jnp.dot(weights, values, preferred_element_type=jnp.float32)
        denominator = jnp.sum(weights.astype(jnp.float32), axis=1, keepdims=True)
        parts.append((numerator, denominator))
    num_out[...] = num_in[...] + jnp.where(first, parts[0][0], parts[1][0])
    den_out[...] = den_in[...] + jnp.where(first, parts[0][1], parts[1][1])


def heads_norm_kernel(proj_ref, q_gain_ref, k_gain_ref, q_ref, kv_ref, *, head_size, width):
    first = lax.broadcasted_iota(jnp.int32, (1, 2 * head_size), 1) < head_size

    def head_norm(values, gain):
        def head_mean(x):
            total_a = jnp.sum(jnp.where(first, x, 0.0), axis=1, keepdims=True)
            total_b = jnp.sum(jnp.where(first, 0.0, x), axis=1, keepdims=True)
            return jnp.where(first, total_a, total_b) / head_size

        centred = values - head_mean(values)
        spread = head_mean(centred * centred)
        return centred * lax.rsqrt(spread + 1e-06) * gain

    for pair in range(width // (2 * head_size)):
        lanes = slice(pair * 2 * head_size, (pair + 1) * 2 * head_size)
        q_ref[:, lanes] = head_norm(proj_ref[:, lanes], q_gain_ref[...]).astype(q_ref.dtype)
        key_lanes = slice(width + lanes.start, width + lanes.stop)
        kv_ref[0, :, lanes] = head_norm(proj_ref[:, key_lanes], k_gain_ref[...]).astype(kv_ref.dtype)
        value_lanes = slice(2 * width + lanes.start, 2 * width + lanes.stop)
        kv_ref[1, :, lanes] = proj_ref[:, value_lanes].astype(kv_ref.dtype)


def heads_norm(projected, q_gain, k_gain, head_size):
    rows, triple = projected.shape
    width = triple // 3
    tile = min(rows, 256)
    pair_gain = lambda gain: jnp.tile(gain, 2).reshape(1, 2 * head_size)
    gain_spec = pl.BlockSpec((1, 2 * head_size), lambda i: (0, 0))
    return pl.pallas_call(
        functools.partial(heads_norm_kernel, head_size=head_size, width=width),
        grid=(rows // tile,),
        in_specs=[pl.BlockSpec((tile, triple), lambda i: (i, 0)), gain_spec, gain_spec],
        out_specs=[
            pl.BlockSpec((tile, width), lambda i: (i, 0)),
            pl.BlockSpec((2, tile, width), lambda i: (0, i, 0)),
        ],
        out_shape=[
            jax.ShapeDtypeStruct((rows, width), jnp.bfloat16),
            jax.ShapeDtypeStruct((2, rows, width), jnp.bfloat16),
        ],
        cost_estimate=pl.CostEstimate(
            flops=rows * triple * 8, transcendentals=rows * width, bytes_accessed=rows * triple * 6
        ),
    )(projected, pair_gain(q_gain), pair_gain(k_gain))


def attend_block(queries, held, numerator, denominator, row_start, row_count, head_size, scale):
    token_count, width = queries.shape
    key_count = held.shape[1]
    pair_width = 2 * head_size
    tile = min(row_count, 512)
    first_tile = row_start // tile
    row_spec = pl.BlockSpec((tile, pair_width), lambda i, j: (i + first_tile, j))
    key_spec = pl.BlockSpec((None, key_count, pair_width), lambda i, j: (0, 0, j))
    value_spec = pl.BlockSpec((None, key_count, pair_width), lambda i, j: (1, 0, j))
    flops = 2 * 2 * 2 * row_count * key_count * width
    return pl.pallas_call(
        functools.partial(attention_kernel, head_size=head_size, scale=scale),
        grid=(row_count // tile, width // pair_width),
        in_specs=[row_spec, key_spec, value_spec, row_spec, row_spec],
        out_specs=[row_spec, row_spec],
        out_shape=[jax.ShapeDtypeStruct((token_count, width), jnp.float32)] * 2,
        input_output_aliases={3: 0, 4: 1},
        compiler_params=pltpu.CompilerParams(dimension_semantics=("arbitrary", "arbitrary")),
        cost_estimate=pl.CostEstimate(
            flops=flops,
            transcendentals=row_count * key_count * (width // head_size),
            bytes_accessed=row_count * width * 18 + key_count * width * 4 * (row_count // tile),
        ),
    )(queries, held, held, numerator, denominator)


def body(tokens, norm_gain, w_qkv, q_gain, k_gain, w_out, covis_mask, capture_rank):
    full_width = tokens.shape[2]
    local_width = w_qkv.shape[2]
    head_size = q_gain.shape[0]
    heads_here = local_width // head_size
    score_scale = head_size ** (-0.5)
    slab_count = lax.axis_size("slab")
    my_group = lax.axis_index("group")
    group_count = lax.axis_size("group")
    normed = norm_rows(tokens[0].astype(jnp.float32), norm_gain).astype(jnp.bfloat16)
    piece_rows = normed.shape[0]
    flat_w = w_qkv.reshape(full_width, 3 * local_width)

    def project(rows):
        projected = jnp.dot(rows, flat_w, preferred_element_type=jnp.float32)
        return heads_norm(projected, q_gain, k_gain, head_size)

    own_q, own_pairs = project(normed)

    def allowed_from(source):
        in_range = (source >= 0) & (source < group_count)
        clipped = jnp.clip(source, 0, group_count - 1)
        return (
            in_range
            & (covis_mask[my_group, clipped] == 1)
            & (capture_rank[clipped] <= capture_rank[my_group])
        )

    def routed(block, route):
        return lax.ppermute(block, "group", [(a, b) for a, b in route if 0 <= b < group_count])

    g_all = range(group_count)
    spot = my_group % 4
    on_chip = [(g, g ^ 1) for g in g_all]
    across_x = [(g, g ^ 2) for g in g_all]
    along_z_once = [(g, g + 3) if g % 2 == 1 else (g, g - 3) for g in g_all]
    along_z_relay = [(g, g + 4) if g % 4 < 2 else (g, g - 4) for g in g_all]

    def round_one(buf):
        return [
            (my_group ^ 1, routed(buf, on_chip)),
            (my_group ^ 2, routed(buf, across_x)),
            (jnp.where(spot % 2 == 0, my_group - 3, my_group + 3), routed(buf, along_z_once)),
        ]

    def round_two(first):
        from_x = first[1][1]
        return [
            (my_group ^ 3, routed(from_x, on_chip)),
            (jnp.where(spot < 2, my_group - 2, my_group + 2), routed(from_x, along_z_relay)),
        ]

    def round_three(second):
        source = jnp.where(
            spot == 0,
            my_group - 1,
            jnp.where(spot == 1, my_group - 3, jnp.where(spot == 2, my_group + 3, my_group + 1)),
        )
        return [(source, routed(second[1][1], on_chip))]

    queries, pairs = own_q, own_pairs
    w_pieces = [w_out]
    if slab_count > 1:
        gathered = [rotated(normed, "slab", k) for k in range(1, slab_count)]
        w_later = lax.optimization_barrier((w_out, gathered))[0]
        w_pieces += [rotated(w_later, "slab", -k) for k in range(1, slab_count)]
        rest_q, rest_pairs = project(jnp.concatenate(gathered, axis=0))
        queries = jnp.concatenate([own_q, rest_q], axis=0)
        pairs = jnp.concatenate([own_pairs, rest_pairs], axis=1)
    token_count = queries.shape[0]

    def add_terms(held, sums, row_start=0, row_count=None):
        row_count = token_count if row_count is None else row_count
        return tuple(
            attend_block(queries, held, sums[0], sums[1], row_start, row_count, head_size, score_scale)
        )

    def add_masked(arrived, sums, row_start=0, row_count=None):
        for source, held in arrived:
            sums = lax.cond(
                allowed_from(source),
                lambda: add_terms(held, sums, row_start, row_count),
                lambda: sums,
            )
        return sums

    zeros = jnp.zeros((token_count, local_width), jnp.float32)
    first = round_one(pairs)
    sums = add_terms(pairs, (zeros, zeros))
    first, sums = lax.optimization_barrier((first, sums))
    second = round_two(first)
    sums = add_masked(first, sums)
    second, sums = lax.optimization_barrier((second, sums))
    last = round_three(second)
    sums = add_masked(second, sums)
    last, sums = lax.optimization_barrier((last, sums))

    att_pieces = [None] * slab_count
    for k in list(range(1, slab_count)) + [0]:
        row_start = k * piece_rows
        sums = add_masked(last, sums, row_start, piece_rows)
        rows = slice(row_start, row_start + piece_rows)
        attended = (sums[0][rows] / sums[1][rows]).astype(jnp.bfloat16)
        if k != 0:
            attended, last, sums = lax.optimization_barrier((attended, last, sums))
            attended = rotated(attended, "slab", -k)
        att_pieces[k] = attended
    mixed = jnp.dot(
        jnp.concatenate(att_pieces, axis=1),
        jnp.concatenate(w_pieces, axis=0),
        preferred_element_type=jnp.float32,
    )
    return mixed.astype(jnp.bfloat16)[None]


def solution(mesh):
    placed = (
        P("group", "slab", None),
        P(),
        P(None, None, "slab"),
        P(),
        P(),
        P("slab", None),
        P(),
        P(),
    )
    return jax.shard_map(
        body, mesh=mesh, in_specs=placed, out_specs=P("group", "slab", None), check_vma=False
    )
```

```python
import functools

import jax
import jax.numpy as jnp
from jax import lax
from jax.sharding import PartitionSpec as P
from jax.experimental import pallas as pl
from jax.experimental.pallas import tpu as pltpu

REACH = 3


def shifted(block, axis, distance):
    devices = range(lax.axis_size(axis))
    route = [(i - distance, i) for i in devices if i - distance in devices]
    return lax.ppermute(block, axis, route)


def rotated(block, axis, distance):
    count = lax.axis_size(axis)
    route = [(i, (i + distance) % count) for i in range(count)]
    return lax.ppermute(block, axis, route)


def norm_rows(values, gain):
    centre = jnp.mean(values, axis=-1, keepdims=True)
    centred = values - centre
    spread = jnp.mean(centred * centred, axis=-1, keepdims=True)
    return centred * lax.rsqrt(spread + 1e-06) * gain


def block_terms(queries, key_rows, values, score_scale):
    scores = (
        jnp.einsum("qhd,khd->hqk", queries, key_rows, preferred_element_type=jnp.float32)
        * score_scale
    )
    weights = jnp.exp(scores).astype(jnp.bfloat16)
    numerator = jnp.einsum("hqk,khd->qhd", weights, values, preferred_element_type=jnp.float32)
    denominator = jnp.transpose(jnp.sum(weights, axis=2, dtype=jnp.float32))
    return (numerator, denominator)


def attention_kernel(q_ref, k_ref, v_ref, num_in, den_in, num_out, den_out, *, head_size, scale):
    queries = q_ref[...]
    keys = k_ref[...]
    values = v_ref[...]
    first = lax.broadcasted_iota(jnp.int32, (1, 2 * head_size), 1) < head_size
    parts = []
    for lanes in (first, jnp.logical_not(first)):
        head_keys = jnp.where(lanes, keys, jnp.zeros_like(keys))
        scores = lax.dot_general(
            queries, head_keys, (((1,), (1,)), ((), ())), preferred_element_type=jnp.float32
        ) * scale
        weights = jnp.exp(scores).astype(jnp.bfloat16)
        numerator = jnp.dot(weights, values, preferred_element_type=jnp.float32)
        denominator = jnp.sum(weights.astype(jnp.float32), axis=1, keepdims=True)
        parts.append((numerator, denominator))
    num_out[...] = num_in[...] + jnp.where(first, parts[0][0], parts[1][0])
    den_out[...] = den_in[...] + jnp.where(first, parts[0][1], parts[1][1])


def project_kernel(x_ref, w_ref, q_gain_ref, k_gain_ref, q_ref, kv_ref, *, head_size, width):
    first = lax.broadcasted_iota(jnp.int32, (1, 2 * head_size), 1) < head_size

    def head_norm(values, gain):
        def head_mean(x):
            total_a = jnp.sum(jnp.where(first, x, 0.0), axis=1, keepdims=True)
            total_b = jnp.sum(jnp.where(first, 0.0, x), axis=1, keepdims=True)
            return jnp.where(first, total_a, total_b) / head_size

        centred = values - head_mean(values)
        spread = head_mean(centred * centred)
        return centred * lax.rsqrt(spread + 1e-06) * gain

    rows = x_ref[...]
    for part in range(3):
        projected = jnp.dot(
            rows, w_ref[part], preferred_element_type=jnp.float32
        )
        for pair in range(width // (2 * head_size)):
            lanes = slice(pair * 2 * head_size, (pair + 1) * 2 * head_size)
            if part == 0:
                q_ref[:, lanes] = head_norm(projected[:, lanes], q_gain_ref[...]).astype(q_ref.dtype)
            elif part == 1:
                kv_ref[0, :, lanes] = head_norm(projected[:, lanes], k_gain_ref[...]).astype(kv_ref.dtype)
            else:
                kv_ref[1, :, lanes] = projected[:, lanes].astype(kv_ref.dtype)


def project_heads(rows, part_w, q_gain, k_gain, head_size):
    row_count, full_width = rows.shape
    width = part_w.shape[2]
    tile = 256 if row_count % 256 == 0 else 128
    pair_gain = lambda gain: jnp.tile(gain, 2).reshape(1, 2 * head_size)
    gain_spec = pl.BlockSpec((1, 2 * head_size), lambda i: (0, 0))
    return pl.pallas_call(
        functools.partial(project_kernel, head_size=head_size, width=width),
        grid=(row_count // tile,),
        in_specs=[
            pl.BlockSpec((tile, full_width), lambda i: (i, 0)),
            pl.BlockSpec((3, full_width, width), lambda i: (0, 0, 0)),
            gain_spec,
            gain_spec,
        ],
        out_specs=[
            pl.BlockSpec((tile, width), lambda i: (i, 0)),
            pl.BlockSpec((2, tile, width), lambda i: (0, i, 0)),
        ],
        out_shape=[
            jax.ShapeDtypeStruct((row_count, width), jnp.bfloat16),
            jax.ShapeDtypeStruct((2, row_count, width), jnp.bfloat16),
        ],
        cost_estimate=pl.CostEstimate(
            flops=2 * row_count * full_width * 3 * width,
            transcendentals=row_count * width,
            bytes_accessed=row_count * full_width * 2 + full_width * 6 * width + row_count * width * 6,
        ),
    )(rows, part_w, pair_gain(q_gain), pair_gain(k_gain))


def attend_block(queries, held, numerator, denominator, row_start, row_count, head_size, scale):
    token_count, width = queries.shape
    key_count = held.shape[1]
    pair_width = 2 * head_size
    tile = min(row_count, 512)
    first_tile = row_start // tile
    row_spec = pl.BlockSpec((tile, pair_width), lambda i, j: (i + first_tile, j))
    key_spec = pl.BlockSpec((None, key_count, pair_width), lambda i, j: (0, 0, j))
    value_spec = pl.BlockSpec((None, key_count, pair_width), lambda i, j: (1, 0, j))
    flops = 2 * 2 * 2 * row_count * key_count * width
    return pl.pallas_call(
        functools.partial(attention_kernel, head_size=head_size, scale=scale),
        grid=(row_count // tile, width // pair_width),
        in_specs=[row_spec, key_spec, value_spec, row_spec, row_spec],
        out_specs=[row_spec, row_spec],
        out_shape=[jax.ShapeDtypeStruct((token_count, width), jnp.float32)] * 2,
        input_output_aliases={3: 0, 4: 1},
        compiler_params=pltpu.CompilerParams(dimension_semantics=("arbitrary", "arbitrary")),
        cost_estimate=pl.CostEstimate(
            flops=flops,
            transcendentals=row_count * key_count * (width // head_size),
            bytes_accessed=row_count * width * 18 + key_count * width * 4 * (row_count // tile),
        ),
    )(queries, held, held, numerator, denominator)


def body(tokens, norm_gain, w_qkv, q_gain, k_gain, w_out, covis_mask, capture_rank):
    full_width = tokens.shape[2]
    local_width = w_qkv.shape[2]
    head_size = q_gain.shape[0]
    heads_here = local_width // head_size
    score_scale = head_size ** (-0.5)
    slab_count = lax.axis_size("slab")
    my_group = lax.axis_index("group")
    group_count = lax.axis_size("group")
    normed = norm_rows(tokens[0].astype(jnp.float32), norm_gain).astype(jnp.bfloat16)
    piece_rows = normed.shape[0]
    part_w = jnp.transpose(w_qkv, (1, 0, 2))

    def project(rows):
        return project_heads(rows, part_w, q_gain, k_gain, head_size)

    own_q, own_pairs = project(normed)

    def allowed_from(source):
        in_range = (source >= 0) & (source < group_count)
        clipped = jnp.clip(source, 0, group_count - 1)
        return (
            in_range
            & (covis_mask[my_group, clipped] == 1)
            & (capture_rank[clipped] <= capture_rank[my_group])
        )

    def routed(block, route):
        return lax.ppermute(block, "group", [(a, b) for a, b in route if 0 <= b < group_count])

    g_all = range(group_count)
    spot = my_group % 4
    on_chip = [(g, g ^ 1) for g in g_all]
    across_x = [(g, g ^ 2) for g in g_all]
    along_z_once = [(g, g + 3) if g % 2 == 1 else (g, g - 3) for g in g_all]
    along_z_relay = [(g, g + 4) if g % 4 < 2 else (g, g - 4) for g in g_all]

    def round_one(buf):
        return [
            (my_group ^ 1, routed(buf, on_chip)),
            (my_group ^ 2, routed(buf, across_x)),
            (jnp.where(spot % 2 == 0, my_group - 3, my_group + 3), routed(buf, along_z_once)),
        ]

    def round_two(first):
        from_x = first[1][1]
        return [
            (my_group ^ 3, routed(from_x, on_chip)),
            (jnp.where(spot < 2, my_group - 2, my_group + 2), routed(from_x, along_z_relay)),
        ]

    def round_three(second):
        source = jnp.where(
            spot == 0,
            my_group - 1,
            jnp.where(spot == 1, my_group - 3, jnp.where(spot == 2, my_group + 3, my_group + 1)),
        )
        return [(source, routed(second[1][1], on_chip))]

    queries, pairs = own_q, own_pairs
    w_pieces = [w_out]
    if slab_count > 1:
        gathered = [rotated(normed, "slab", k) for k in range(1, slab_count)]
        w_later = lax.optimization_barrier((w_out, gathered))[0]
        w_pieces = w_pieces + [rotated(w_later, "slab", -k) for k in range(1, slab_count)]
        rest_q, rest_pairs = project(jnp.concatenate(gathered, axis=0))
        queries = jnp.concatenate([own_q, rest_q], axis=0)
        pairs = jnp.concatenate([own_pairs, rest_pairs], axis=1)
    token_count = queries.shape[0]

    def add_terms(held, sums, row_start=0, row_count=None):
        row_count = token_count if row_count is None else row_count
        return tuple(
            attend_block(queries, held, sums[0], sums[1], row_start, row_count, head_size, score_scale)
        )

    def add_masked(arrived, sums, row_start=0, row_count=None):
        for source, held in arrived:
            sums = lax.cond(
                allowed_from(source),
                lambda: add_terms(held, sums, row_start, row_count),
                lambda: sums,
            )
        return sums

    zeros = jnp.zeros((token_count, local_width), jnp.float32)
    first = round_one(pairs)
    sums = add_terms(pairs, (zeros, zeros))
    first, sums, w_pieces = lax.optimization_barrier((first, sums, w_pieces))
    second = round_two(first)
    sums = add_masked(first, sums)
    second, sums = lax.optimization_barrier((second, sums))
    last = round_three(second)
    sums = add_masked(second, sums)
    last, sums = lax.optimization_barrier((last, sums))

    att_pieces = [None] * slab_count
    for k in list(range(1, slab_count)) + [0]:
        row_start = k * piece_rows
        sums = add_masked(last, sums, row_start, piece_rows)
        rows = slice(row_start, row_start + piece_rows)
        attended = (sums[0][rows] / sums[1][rows]).astype(jnp.bfloat16)
        if k != 0:
            attended, last, sums = lax.optimization_barrier((attended, last, sums))
            attended = rotated(attended, "slab", -k)
        att_pieces[k] = attended
    mixed = jnp.dot(
        jnp.concatenate(att_pieces, axis=1),
        jnp.concatenate(w_pieces, axis=0),
        preferred_element_type=jnp.float32,
    )
    return mixed.astype(jnp.bfloat16)[None]


def solution(mesh):
    placed = (
        P("group", "slab", None),
        P(),
        P(None, None, "slab"),
        P(),
        P(),
        P("slab", None),
        P(),
        P(),
    )
    return jax.shard_map(
        body, mesh=mesh, in_specs=placed, out_specs=P("group", "slab", None), check_vma=False
    )
```

```python
import functools

import jax
import jax.numpy as jnp
from jax import lax
from jax.sharding import PartitionSpec as P
from jax.experimental import pallas as pl
from jax.experimental.pallas import tpu as pltpu

REACH = 3


def shifted(block, axis, distance):
    devices = range(lax.axis_size(axis))
    route = [(i - distance, i) for i in devices if i - distance in devices]
    return lax.ppermute(block, axis, route)


def rotated(block, axis, distance):
    count = lax.axis_size(axis)
    route = [(i, (i + distance) % count) for i in range(count)]
    return lax.ppermute(block, axis, route)


def norm_rows(values, gain):
    centre = jnp.mean(values, axis=-1, keepdims=True)
    centred = values - centre
    spread = jnp.mean(centred * centred, axis=-1, keepdims=True)
    return centred * lax.rsqrt(spread + 1e-06) * gain


def block_terms(queries, key_rows, values, score_scale):
    scores = (
        jnp.einsum("qhd,khd->hqk", queries, key_rows, preferred_element_type=jnp.float32)
        * score_scale
    )
    weights = jnp.exp(scores).astype(jnp.bfloat16)
    numerator = jnp.einsum("hqk,khd->qhd", weights, values, preferred_element_type=jnp.float32)
    denominator = jnp.transpose(jnp.sum(weights, axis=2, dtype=jnp.float32))
    return (numerator, denominator)


def attention_kernel(q_ref, k_ref, v_ref, num_in, den_in, num_out, den_out, *, head_size, scale):
    queries = q_ref[...]
    keys = k_ref[...]
    values = v_ref[...]
    first = lax.broadcasted_iota(jnp.int32, (1, 2 * head_size), 1) < head_size
    parts = []
    for lanes in (first, jnp.logical_not(first)):
        head_keys = jnp.where(lanes, keys, jnp.zeros_like(keys))
        scores = lax.dot_general(
            queries, head_keys, (((1,), (1,)), ((), ())), preferred_element_type=jnp.float32
        ) * scale
        weights = jnp.exp(scores).astype(jnp.bfloat16)
        numerator = jnp.dot(weights, values, preferred_element_type=jnp.float32)
        denominator = jnp.sum(weights.astype(jnp.float32), axis=1, keepdims=True)
        parts.append((numerator, denominator))
    num_out[...] = num_in[...] + jnp.where(first, parts[0][0], parts[1][0])
    den_out[...] = den_in[...] + jnp.where(first, parts[0][1], parts[1][1])


def project_kernel(x_ref, w_ref, q_gain_ref, k_gain_ref, q_ref, kv_ref, *, head_size, width):
    first = lax.broadcasted_iota(jnp.int32, (1, 2 * head_size), 1) < head_size

    def head_norm(values, gain):
        def head_mean(x):
            total_a = jnp.sum(jnp.where(first, x, 0.0), axis=1, keepdims=True)
            total_b = jnp.sum(jnp.where(first, 0.0, x), axis=1, keepdims=True)
            return jnp.where(first, total_a, total_b) / head_size

        centred = values - head_mean(values)
        spread = head_mean(centred * centred)
        return centred * lax.rsqrt(spread + 1e-06) * gain

    rows = x_ref[...]
    for part in range(3):
        projected = jnp.dot(
            rows, w_ref[part], preferred_element_type=jnp.float32
        )
        for pair in range(width // (2 * head_size)):
            lanes = slice(pair * 2 * head_size, (pair + 1) * 2 * head_size)
            if part == 0:
                q_ref[:, lanes] = head_norm(projected[:, lanes], q_gain_ref[...]).astype(q_ref.dtype)
            elif part == 1:
                kv_ref[0, :, lanes] = head_norm(projected[:, lanes], k_gain_ref[...]).astype(kv_ref.dtype)
            else:
                kv_ref[1, :, lanes] = projected[:, lanes].astype(kv_ref.dtype)


def project_heads(rows, part_w, q_gain, k_gain, head_size):
    row_count, full_width = rows.shape
    width = part_w.shape[2]
    tile = 256 if row_count % 256 == 0 else 128
    pair_gain = lambda gain: jnp.tile(gain, 2).reshape(1, 2 * head_size)
    gain_spec = pl.BlockSpec((1, 2 * head_size), lambda i: (0, 0))
    return pl.pallas_call(
        functools.partial(project_kernel, head_size=head_size, width=width),
        grid=(row_count // tile,),
        in_specs=[
            pl.BlockSpec((tile, full_width), lambda i: (i, 0)),
            pl.BlockSpec((3, full_width, width), lambda i: (0, 0, 0)),
            gain_spec,
            gain_spec,
        ],
        out_specs=[
            pl.BlockSpec((tile, width), lambda i: (i, 0)),
            pl.BlockSpec((2, tile, width), lambda i: (0, i, 0)),
        ],
        out_shape=[
            jax.ShapeDtypeStruct((row_count, width), jnp.bfloat16),
            jax.ShapeDtypeStruct((2, row_count, width), jnp.bfloat16),
        ],
        cost_estimate=pl.CostEstimate(
            flops=2 * row_count * full_width * 3 * width,
            transcendentals=row_count * width,
            bytes_accessed=row_count * full_width * 2 + full_width * 6 * width + row_count * width * 6,
        ),
    )(rows, part_w, pair_gain(q_gain), pair_gain(k_gain))


def attend_block(queries, held, numerator, denominator, row_start, row_count, head_size, scale):
    token_count, width = queries.shape
    key_count = held.shape[1]
    pair_width = 2 * head_size
    tile = min(row_count, 512)
    first_tile = row_start // tile
    row_spec = pl.BlockSpec((tile, pair_width), lambda i, j: (i + first_tile, j))
    key_spec = pl.BlockSpec((None, key_count, pair_width), lambda i, j: (0, 0, j))
    value_spec = pl.BlockSpec((None, key_count, pair_width), lambda i, j: (1, 0, j))
    flops = 2 * 2 * 2 * row_count * key_count * width
    return pl.pallas_call(
        functools.partial(attention_kernel, head_size=head_size, scale=scale),
        grid=(row_count // tile, width // pair_width),
        in_specs=[row_spec, key_spec, value_spec, row_spec, row_spec],
        out_specs=[row_spec, row_spec],
        out_shape=[jax.ShapeDtypeStruct((token_count, width), jnp.float32)] * 2,
        input_output_aliases={3: 0, 4: 1},
        compiler_params=pltpu.CompilerParams(dimension_semantics=("arbitrary", "arbitrary")),
        cost_estimate=pl.CostEstimate(
            flops=flops,
            transcendentals=row_count * key_count * (width // head_size),
            bytes_accessed=row_count * width * 18 + key_count * width * 4 * (row_count // tile),
        ),
    )(queries, held, held, numerator, denominator)


def body(tokens, norm_gain, w_qkv, q_gain, k_gain, w_out, covis_mask, capture_rank):
    full_width = tokens.shape[2]
    local_width = w_qkv.shape[2]
    head_size = q_gain.shape[0]
    heads_here = local_width // head_size
    score_scale = head_size ** (-0.5)
    slab_count = lax.axis_size("slab")
    my_group = lax.axis_index("group")
    group_count = lax.axis_size("group")
    normed = norm_rows(tokens[0].astype(jnp.float32), norm_gain).astype(jnp.bfloat16)
    piece_rows = normed.shape[0]
    part_w = jnp.transpose(w_qkv, (1, 0, 2))

    def project(rows):
        return project_heads(rows, part_w, q_gain, k_gain, head_size)

    own_q, own_pairs = project(normed)

    def allowed_from(source):
        in_range = (source >= 0) & (source < group_count)
        clipped = jnp.clip(source, 0, group_count - 1)
        return (
            in_range
            & (covis_mask[my_group, clipped] == 1)
            & (capture_rank[clipped] <= capture_rank[my_group])
        )

    def routed(block, route):
        return lax.ppermute(block, "group", [(a, b) for a, b in route if 0 <= b < group_count])

    g_all = range(group_count)
    spot = my_group % 4
    on_chip = [(g, g ^ 1) for g in g_all]
    across_x = [(g, g ^ 2) for g in g_all]
    along_z_once = [(g, g + 3) if g % 2 == 1 else (g, g - 3) for g in g_all]
    mixed_relay = [
        (g, g ^ 2) if g % 4 in (1, 2) else ((g, g + 5) if g % 4 == 0 else (g, g - 5)) for g in g_all
    ]

    def round_one(buf):
        return [
            (my_group ^ 1, routed(buf, on_chip)),
            (my_group ^ 2, routed(buf, across_x)),
            (jnp.where(spot % 2 == 0, my_group - 3, my_group + 3), routed(buf, along_z_once)),
        ]

    def round_two(first):
        from_x, from_z = first[1][1], first[2][1]
        outgoing = jnp.where((spot == 1) | (spot == 2), from_z, from_x)
        source = jnp.where(
            spot == 0,
            my_group - 1,
            jnp.where(spot == 1, my_group - 3, jnp.where(spot == 2, my_group + 3, my_group + 1)),
        )
        return [
            (my_group ^ 3, routed(from_x, on_chip)),
            (source, routed(outgoing, mixed_relay)),
        ]

    def round_three(second):
        return [(jnp.where(spot < 2, my_group - 2, my_group + 2), routed(second[1][1], on_chip))]

    queries, pairs = own_q, own_pairs
    w_pieces = [w_out]
    if slab_count > 1:
        gathered = [rotated(normed, "slab", k) for k in range(1, slab_count)]
        w_later = lax.optimization_barrier((w_out, gathered))[0]
        w_pieces = w_pieces + [rotated(w_later, "slab", -k) for k in range(1, slab_count)]
        rest_q, rest_pairs = project(jnp.concatenate(gathered, axis=0))
        queries = jnp.concatenate([own_q, rest_q], axis=0)
        pairs = jnp.concatenate([own_pairs, rest_pairs], axis=1)
    token_count = queries.shape[0]

    def add_terms(held, sums, row_start=0, row_count=None):
        row_count = token_count if row_count is None else row_count
        return tuple(
            attend_block(queries, held, sums[0], sums[1], row_start, row_count, head_size, score_scale)
        )

    def add_masked(arrived, sums, row_start=0, row_count=None):
        for source, held in arrived:
            sums = lax.cond(
                allowed_from(source),
                lambda: add_terms(held, sums, row_start, row_count),
                lambda: sums,
            )
        return sums

    zeros = jnp.zeros((token_count, local_width), jnp.float32)
    first = round_one(pairs)
    sums = add_terms(pairs, (zeros, zeros))
    first, sums, w_pieces = lax.optimization_barrier((first, sums, w_pieces))
    second = round_two(first)
    sums = add_masked(first, sums)
    second, sums = lax.optimization_barrier((second, sums))
    last = round_three(second)
    sums = add_masked(second, sums)
    last, sums = lax.optimization_barrier((last, sums))

    att_pieces = [None] * slab_count
    for k in list(range(1, slab_count)) + [0]:
        row_start = k * piece_rows
        sums = add_masked(last, sums, row_start, piece_rows)
        rows = slice(row_start, row_start + piece_rows)
        attended = (sums[0][rows] / sums[1][rows]).astype(jnp.bfloat16)
        if k != 0:
            attended, last, sums = lax.optimization_barrier((attended, last, sums))
            attended = rotated(attended, "slab", -k)
        att_pieces[k] = attended
    mixed = jnp.dot(
        jnp.concatenate(att_pieces, axis=1),
        jnp.concatenate(w_pieces, axis=0),
        preferred_element_type=jnp.float32,
    )
    return mixed.astype(jnp.bfloat16)[None]


def solution(mesh):
    placed = (
        P("group", "slab", None),
        P(),
        P(None, None, "slab"),
        P(),
        P(),
        P("slab", None),
        P(),
        P(),
    )
    return jax.shard_map(
        body, mesh=mesh, in_specs=placed, out_specs=P("group", "slab", None), check_vma=False
    )
```

```python
import functools

import jax
import jax.numpy as jnp
from jax import lax
from jax.sharding import PartitionSpec as P
from jax.experimental import pallas as pl
from jax.experimental.pallas import tpu as pltpu

REACH = 3


def shifted(block, axis, distance):
    devices = range(lax.axis_size(axis))
    route = [(i - distance, i) for i in devices if i - distance in devices]
    return lax.ppermute(block, axis, route)


def rotated(block, axis, distance):
    count = lax.axis_size(axis)
    route = [(i, (i + distance) % count) for i in range(count)]
    return lax.ppermute(block, axis, route)


def norm_rows(values, gain):
    centre = jnp.mean(values, axis=-1, keepdims=True)
    centred = values - centre
    spread = jnp.mean(centred * centred, axis=-1, keepdims=True)
    return centred * lax.rsqrt(spread + 1e-06) * gain


def block_terms(queries, key_rows, values, score_scale):
    scores = (
        jnp.einsum("qhd,khd->hqk", queries, key_rows, preferred_element_type=jnp.float32)
        * score_scale
    )
    weights = jnp.exp(scores).astype(jnp.bfloat16)
    numerator = jnp.einsum("hqk,khd->qhd", weights, values, preferred_element_type=jnp.float32)
    denominator = jnp.transpose(jnp.sum(weights, axis=2, dtype=jnp.float32))
    return (numerator, denominator)


def attention_kernel(q_ref, k_ref, v_ref, num_in, den_in, num_out, den_out, *, head_size, scale):
    queries = q_ref[...]
    keys = k_ref[...]
    values = v_ref[...]
    first = lax.broadcasted_iota(jnp.int32, (1, 2 * head_size), 1) < head_size
    parts = []
    for lanes in (first, jnp.logical_not(first)):
        head_keys = jnp.where(lanes, keys, jnp.zeros_like(keys))
        scores = lax.dot_general(
            queries, head_keys, (((1,), (1,)), ((), ())), preferred_element_type=jnp.float32
        ) * scale
        weights = jnp.exp(scores).astype(jnp.bfloat16)
        numerator = jnp.dot(weights, values, preferred_element_type=jnp.float32)
        denominator = jnp.sum(weights.astype(jnp.float32), axis=1, keepdims=True)
        parts.append((numerator, denominator))
    num_out[...] = num_in[...] + jnp.where(first, parts[0][0], parts[1][0])
    den_out[...] = den_in[...] + jnp.where(first, parts[0][1], parts[1][1])


def project_kernel(x_ref, w_ref, q_gain_ref, k_gain_ref, q_in, kv_in, q_ref, kv_ref, *, head_size, width):
    first = lax.broadcasted_iota(jnp.int32, (1, 2 * head_size), 1) < head_size

    def head_norm(values, gain):
        def head_mean(x):
            total_a = jnp.sum(jnp.where(first, x, 0.0), axis=1, keepdims=True)
            total_b = jnp.sum(jnp.where(first, 0.0, x), axis=1, keepdims=True)
            return jnp.where(first, total_a, total_b) / head_size

        centred = values - head_mean(values)
        spread = head_mean(centred * centred)
        return centred * lax.rsqrt(spread + 1e-06) * gain

    rows = x_ref[...]
    for part in range(3):
        projected = jnp.dot(
            rows, w_ref[part], preferred_element_type=jnp.float32
        )
        for pair in range(width // (2 * head_size)):
            lanes = slice(pair * 2 * head_size, (pair + 1) * 2 * head_size)
            if part == 0:
                q_ref[:, lanes] = head_norm(projected[:, lanes], q_gain_ref[...]).astype(q_ref.dtype)
            elif part == 1:
                kv_ref[0, :, lanes] = head_norm(projected[:, lanes], k_gain_ref[...]).astype(kv_ref.dtype)
            else:
                kv_ref[1, :, lanes] = projected[:, lanes].astype(kv_ref.dtype)


def project_heads(rows, part_w, q_gain, k_gain, head_size, q_buf, kv_buf, row_start):
    row_count, full_width = rows.shape
    width = part_w.shape[2]
    tile = 256 if row_count % 256 == 0 else 128
    first_tile = row_start // tile
    pair_gain = lambda gain: jnp.tile(gain, 2).reshape(1, 2 * head_size)
    gain_spec = pl.BlockSpec((1, 2 * head_size), lambda i: (0, 0))
    q_spec = pl.BlockSpec((tile, width), lambda i: (i + first_tile, 0))
    kv_spec = pl.BlockSpec((2, tile, width), lambda i: (0, i + first_tile, 0))
    return pl.pallas_call(
        functools.partial(project_kernel, head_size=head_size, width=width),
        grid=(row_count // tile,),
        in_specs=[
            pl.BlockSpec((tile, full_width), lambda i: (i, 0)),
            pl.BlockSpec((3, full_width, width), lambda i: (0, 0, 0)),
            gain_spec,
            gain_spec,
            q_spec,
            kv_spec,
        ],
        out_specs=[q_spec, kv_spec],
        out_shape=[
            jax.ShapeDtypeStruct(q_buf.shape, jnp.bfloat16),
            jax.ShapeDtypeStruct(kv_buf.shape, jnp.bfloat16),
        ],
        input_output_aliases={4: 0, 5: 1},
        cost_estimate=pl.CostEstimate(
            flops=2 * row_count * full_width * 3 * width,
            transcendentals=row_count * width,
            bytes_accessed=row_count * full_width * 2 + full_width * 6 * width + row_count * width * 6,
        ),
    )(rows, part_w, pair_gain(q_gain), pair_gain(k_gain), q_buf, kv_buf)


def attend_block(queries, held, numerator, denominator, row_start, row_count, head_size, scale):
    token_count, width = queries.shape
    key_count = held.shape[1]
    pair_width = 2 * head_size
    tile = min(row_count, 1024)
    first_tile = row_start // tile
    row_spec = pl.BlockSpec((tile, pair_width), lambda i, j: (i + first_tile, j))
    key_spec = pl.BlockSpec((None, key_count, pair_width), lambda i, j: (0, 0, j))
    value_spec = pl.BlockSpec((None, key_count, pair_width), lambda i, j: (1, 0, j))
    flops = 2 * 2 * 2 * row_count * key_count * width
    return pl.pallas_call(
        functools.partial(attention_kernel, head_size=head_size, scale=scale),
        grid=(row_count // tile, width // pair_width),
        in_specs=[row_spec, key_spec, value_spec, row_spec, row_spec],
        out_specs=[row_spec, row_spec],
        out_shape=[jax.ShapeDtypeStruct((token_count, width), jnp.float32)] * 2,
        input_output_aliases={3: 0, 4: 1},
        compiler_params=pltpu.CompilerParams(dimension_semantics=("arbitrary", "arbitrary")),
        cost_estimate=pl.CostEstimate(
            flops=flops,
            transcendentals=row_count * key_count * (width // head_size),
            bytes_accessed=row_count * width * 18 + key_count * width * 4 * (row_count // tile),
        ),
    )(queries, held, held, numerator, denominator)


def body(tokens, norm_gain, w_qkv, q_gain, k_gain, w_out, covis_mask, capture_rank):
    full_width = tokens.shape[2]
    local_width = w_qkv.shape[2]
    head_size = q_gain.shape[0]
    heads_here = local_width // head_size
    score_scale = head_size ** (-0.5)
    slab_count = lax.axis_size("slab")
    my_group = lax.axis_index("group")
    group_count = lax.axis_size("group")
    normed = norm_rows(tokens[0].astype(jnp.float32), norm_gain).astype(jnp.bfloat16)
    piece_rows = normed.shape[0]
    part_w = jnp.transpose(w_qkv, (1, 0, 2))

    token_count = tokens.shape[1] * slab_count

    def project(rows, buffers, row_start):
        return project_heads(rows, part_w, q_gain, k_gain, head_size, *buffers, row_start)

    empty = (
        jnp.zeros((token_count, local_width), jnp.bfloat16),
        jnp.zeros((2, token_count, local_width), jnp.bfloat16),
    )
    own_q, own_pairs = project(normed, empty, 0)

    def allowed_from(source):
        in_range = (source >= 0) & (source < group_count)
        clipped = jnp.clip(source, 0, group_count - 1)
        return (
            in_range
            & (covis_mask[my_group, clipped] == 1)
            & (capture_rank[clipped] <= capture_rank[my_group])
        )

    def routed(block, route):
        return lax.ppermute(block, "group", [(a, b) for a, b in route if 0 <= b < group_count])

    g_all = range(group_count)
    spot = my_group % 4
    on_chip = [(g, g ^ 1) for g in g_all]
    across_x = [(g, g ^ 2) for g in g_all]
    along_z_once = [(g, g + 3) if g % 2 == 1 else (g, g - 3) for g in g_all]
    mixed_relay = [
        (g, g ^ 2) if g % 4 in (1, 2) else ((g, g + 5) if g % 4 == 0 else (g, g - 5)) for g in g_all
    ]

    def round_one(buf):
        return [
            (my_group ^ 1, routed(buf, on_chip)),
            (my_group ^ 2, routed(buf, across_x)),
            (jnp.where(spot % 2 == 0, my_group - 3, my_group + 3), routed(buf, along_z_once)),
        ]

    def round_two(first):
        from_x, from_z = first[1][1], first[2][1]
        outgoing = jnp.where((spot == 1) | (spot == 2), from_z, from_x)
        source = jnp.where(
            spot == 0,
            my_group - 1,
            jnp.where(spot == 1, my_group - 3, jnp.where(spot == 2, my_group + 3, my_group + 1)),
        )
        return [
            (my_group ^ 3, routed(from_x, on_chip)),
            (source, routed(outgoing, mixed_relay)),
        ]

    def round_three(second):
        return [(jnp.where(spot < 2, my_group - 2, my_group + 2), routed(second[1][1], on_chip))]

    queries, pairs = own_q, own_pairs
    w_pieces = [w_out]
    if slab_count > 1:
        gathered = [rotated(normed, "slab", k) for k in range(1, slab_count)]
        w_later = lax.optimization_barrier((w_out, gathered))[0]
        w_pieces = w_pieces + [rotated(w_later, "slab", -k) for k in range(1, slab_count)]
        queries, pairs = project(jnp.concatenate(gathered, axis=0), (own_q, own_pairs), piece_rows)

    def add_terms(held, sums, row_start=0, row_count=None):
        row_count = token_count if row_count is None else row_count
        return tuple(
            attend_block(queries, held, sums[0], sums[1], row_start, row_count, head_size, score_scale)
        )

    def add_masked(arrived, sums, row_start=0, row_count=None):
        for source, held in arrived:
            sums = lax.cond(
                allowed_from(source),
                lambda: add_terms(held, sums, row_start, row_count),
                lambda: sums,
            )
        return sums

    zeros = jnp.zeros((token_count, local_width), jnp.float32)
    first = round_one(pairs)
    sums = add_terms(pairs, (zeros, zeros))
    first, sums, w_pieces = lax.optimization_barrier((first, sums, w_pieces))
    second = round_two(first)
    sums = add_masked(first, sums)
    second, sums = lax.optimization_barrier((second, sums))
    last = round_three(second)
    sums = add_masked(second, sums)
    last, sums = lax.optimization_barrier((last, sums))

    att_pieces = [None] * slab_count
    for k in list(range(1, slab_count)) + [0]:
        row_start = k * piece_rows
        sums = add_masked(last, sums, row_start, piece_rows)
        rows = slice(row_start, row_start + piece_rows)
        attended = (sums[0][rows] / sums[1][rows]).astype(jnp.bfloat16)
        if k != 0:
            attended, last, sums = lax.optimization_barrier((attended, last, sums))
            attended = rotated(attended, "slab", -k)
        att_pieces[k] = attended
    mixed = jnp.dot(
        jnp.concatenate(att_pieces, axis=1),
        jnp.concatenate(w_pieces, axis=0),
        preferred_element_type=jnp.float32,
    )
    return mixed.astype(jnp.bfloat16)[None]


def solution(mesh):
    placed = (
        P("group", "slab", None),
        P(),
        P(None, None, "slab"),
        P(),
        P(),
        P("slab", None),
        P(),
        P(),
    )
    return jax.shard_map(
        body, mesh=mesh, in_specs=placed, out_specs=P("group", "slab", None), check_vma=False
    )
```

```python
import functools

import jax
import jax.numpy as jnp
from jax import lax
from jax.sharding import PartitionSpec as P
from jax.experimental import pallas as pl
from jax.experimental.pallas import tpu as pltpu

REACH = 3


def shifted(block, axis, distance):
    devices = range(lax.axis_size(axis))
    route = [(i - distance, i) for i in devices if i - distance in devices]
    return lax.ppermute(block, axis, route)


def rotated(block, axis, distance):
    count = lax.axis_size(axis)
    route = [(i, (i + distance) % count) for i in range(count)]
    return lax.ppermute(block, axis, route)


def norm_rows(values, gain):
    centre = jnp.mean(values, axis=-1, keepdims=True)
    centred = values - centre
    spread = jnp.mean(centred * centred, axis=-1, keepdims=True)
    return centred * lax.rsqrt(spread + 1e-06) * gain


def block_terms(queries, key_rows, values, score_scale):
    scores = (
        jnp.einsum("qhd,khd->hqk", queries, key_rows, preferred_element_type=jnp.float32)
        * score_scale
    )
    weights = jnp.exp(scores).astype(jnp.bfloat16)
    numerator = jnp.einsum("hqk,khd->qhd", weights, values, preferred_element_type=jnp.float32)
    denominator = jnp.transpose(jnp.sum(weights, axis=2, dtype=jnp.float32))
    return (numerator, denominator)


def attention_kernel(q_ref, k_ref, v_ref, num_in, den_in, num_out, den_out, *, head_size, scale):
    queries = q_ref[...]
    keys = k_ref[...]
    values = v_ref[...]
    first = lax.broadcasted_iota(jnp.int32, (1, 2 * head_size), 1) < head_size
    parts = []
    for lanes in (first, jnp.logical_not(first)):
        head_keys = jnp.where(lanes, keys, jnp.zeros_like(keys))
        scores = lax.dot_general(
            queries, head_keys, (((1,), (1,)), ((), ())), preferred_element_type=jnp.float32
        ) * scale
        weights = jnp.exp(scores).astype(jnp.bfloat16)
        numerator = jnp.dot(weights, values, preferred_element_type=jnp.float32)
        denominator = jnp.sum(weights.astype(jnp.float32), axis=1, keepdims=True)
        parts.append((numerator, denominator))
    num_out[...] = num_in[...] + jnp.where(first, parts[0][0], parts[1][0])
    den_out[...] = den_in[...] + jnp.where(first, parts[0][1], parts[1][1])


def project_kernel(x_ref, w_ref, q_gain_ref, k_gain_ref, q_in, kv_in, q_ref, kv_ref, piece_ref, *, head_size, width):
    first = lax.broadcasted_iota(jnp.int32, (1, 2 * head_size), 1) < head_size

    def head_norm(values, gain):
        def head_mean(x):
            total_a = jnp.sum(jnp.where(first, x, 0.0), axis=1, keepdims=True)
            total_b = jnp.sum(jnp.where(first, 0.0, x), axis=1, keepdims=True)
            return jnp.where(first, total_a, total_b) / head_size

        centred = values - head_mean(values)
        spread = head_mean(centred * centred)
        return centred * lax.rsqrt(spread + 1e-06) * gain

    rows = x_ref[...]
    for part in range(3):
        projected = jnp.dot(
            rows, w_ref[part], preferred_element_type=jnp.float32
        )
        for pair in range(width // (2 * head_size)):
            lanes = slice(pair * 2 * head_size, (pair + 1) * 2 * head_size)
            if part == 0:
                q_ref[:, lanes] = head_norm(projected[:, lanes], q_gain_ref[...]).astype(q_ref.dtype)
            else:
                if part == 1:
                    block = head_norm(projected[:, lanes], k_gain_ref[...]).astype(kv_ref.dtype)
                else:
                    block = projected[:, lanes].astype(kv_ref.dtype)
                kv_ref[part - 1, :, lanes] = block
                piece_ref[part - 1, :, lanes] = block


def project_heads(rows, part_w, q_gain, k_gain, head_size, q_buf, kv_buf, row_start):
    row_count, full_width = rows.shape
    width = part_w.shape[2]
    tile = 256 if row_count % 256 == 0 else 128
    first_tile = row_start // tile
    pair_gain = lambda gain: jnp.tile(gain, 2).reshape(1, 2 * head_size)
    gain_spec = pl.BlockSpec((1, 2 * head_size), lambda i: (0, 0))
    q_spec = pl.BlockSpec((tile, width), lambda i: (i + first_tile, 0))
    kv_spec = pl.BlockSpec((2, tile, width), lambda i: (0, i + first_tile, 0))
    return pl.pallas_call(
        functools.partial(project_kernel, head_size=head_size, width=width),
        grid=(row_count // tile,),
        in_specs=[
            pl.BlockSpec((tile, full_width), lambda i: (i, 0)),
            pl.BlockSpec((3, full_width, width), lambda i: (0, 0, 0)),
            gain_spec,
            gain_spec,
            q_spec,
            kv_spec,
        ],
        out_specs=[q_spec, kv_spec, pl.BlockSpec((2, tile, width), lambda i: (0, i, 0))],
        out_shape=[
            jax.ShapeDtypeStruct(q_buf.shape, jnp.bfloat16),
            jax.ShapeDtypeStruct(kv_buf.shape, jnp.bfloat16),
            jax.ShapeDtypeStruct((2, row_count, width), jnp.bfloat16),
        ],
        input_output_aliases={4: 0, 5: 1},
        cost_estimate=pl.CostEstimate(
            flops=2 * row_count * full_width * 3 * width,
            transcendentals=row_count * width,
            bytes_accessed=row_count * full_width * 2 + full_width * 6 * width + row_count * width * 6,
        ),
    )(rows, part_w, pair_gain(q_gain), pair_gain(k_gain), q_buf, kv_buf)


def attend_block(queries, held, numerator, denominator, row_start, row_count, head_size, scale):
    token_count, width = queries.shape
    key_count = held.shape[1]
    pair_width = 2 * head_size
    tile = min(row_count, 1024)
    first_tile = row_start // tile
    row_spec = pl.BlockSpec((tile, pair_width), lambda i, j: (i + first_tile, j))
    key_spec = pl.BlockSpec((None, key_count, pair_width), lambda i, j: (0, 0, j))
    value_spec = pl.BlockSpec((None, key_count, pair_width), lambda i, j: (1, 0, j))
    flops = 2 * 2 * 2 * row_count * key_count * width
    return pl.pallas_call(
        functools.partial(attention_kernel, head_size=head_size, scale=scale),
        grid=(row_count // tile, width // pair_width),
        in_specs=[row_spec, key_spec, value_spec, row_spec, row_spec],
        out_specs=[row_spec, row_spec],
        out_shape=[jax.ShapeDtypeStruct((token_count, width), jnp.float32)] * 2,
        input_output_aliases={3: 0, 4: 1},
        compiler_params=pltpu.CompilerParams(dimension_semantics=("arbitrary", "arbitrary")),
        cost_estimate=pl.CostEstimate(
            flops=flops,
            transcendentals=row_count * key_count * (width // head_size),
            bytes_accessed=row_count * width * 18 + key_count * width * 4 * (row_count // tile),
        ),
    )(queries, held, held, numerator, denominator)


def body(tokens, norm_gain, w_qkv, q_gain, k_gain, w_out, covis_mask, capture_rank):
    full_width = tokens.shape[2]
    local_width = w_qkv.shape[2]
    head_size = q_gain.shape[0]
    heads_here = local_width // head_size
    score_scale = head_size ** (-0.5)
    slab_count = lax.axis_size("slab")
    my_group = lax.axis_index("group")
    group_count = lax.axis_size("group")
    normed = norm_rows(tokens[0].astype(jnp.float32), norm_gain).astype(jnp.bfloat16)
    piece_rows = normed.shape[0]
    part_w = jnp.transpose(w_qkv, (1, 0, 2))

    token_count = tokens.shape[1] * slab_count

    def project(rows, buffers, row_start):
        return project_heads(rows, part_w, q_gain, k_gain, head_size, *buffers, row_start)

    empty = (
        jnp.zeros((token_count, local_width), jnp.bfloat16),
        jnp.zeros((2, token_count, local_width), jnp.bfloat16),
    )
    own_q, own_pairs, own_piece = project(normed, empty, 0)

    def allowed_from(source):
        in_range = (source >= 0) & (source < group_count)
        clipped = jnp.clip(source, 0, group_count - 1)
        return (
            in_range
            & (covis_mask[my_group, clipped] == 1)
            & (capture_rank[clipped] <= capture_rank[my_group])
        )

    def routed(block, route):
        return lax.ppermute(block, "group", [(a, b) for a, b in route if 0 <= b < group_count])

    g_all = range(group_count)
    spot = my_group % 4
    on_chip = [(g, g ^ 1) for g in g_all]
    across_x = [(g, g ^ 2) for g in g_all]
    along_z_once = [(g, g + 3) if g % 2 == 1 else (g, g - 3) for g in g_all]
    mixed_relay = [
        (g, g ^ 2) if g % 4 in (1, 2) else ((g, g + 5) if g % 4 == 0 else (g, g - 5)) for g in g_all
    ]

    def round_one(buf, from_x):
        return [
            (my_group ^ 1, routed(buf, on_chip)),
            (my_group ^ 2, from_x),
            (jnp.where(spot % 2 == 0, my_group - 3, my_group + 3), routed(buf, along_z_once)),
        ]

    def round_two(first):
        from_x, from_z = first[1][1], first[2][1]
        outgoing = jnp.where((spot == 1) | (spot == 2), from_z, from_x)
        source = jnp.where(
            spot == 0,
            my_group - 1,
            jnp.where(spot == 1, my_group - 3, jnp.where(spot == 2, my_group + 3, my_group + 1)),
        )
        return [
            (my_group ^ 3, routed(from_x, on_chip)),
            (source, routed(outgoing, mixed_relay)),
        ]

    def round_three(second):
        return [(jnp.where(spot < 2, my_group - 2, my_group + 2), routed(second[1][1], on_chip))]

    early_x = routed(own_piece, across_x)
    queries, pairs = own_q, own_pairs
    w_pieces = [w_out]
    if slab_count > 1:
        gathered = [rotated(normed, "slab", k) for k in range(1, slab_count)]
        w_later = lax.optimization_barrier((w_out, gathered))[0]
        w_pieces = w_pieces + [rotated(w_later, "slab", -k) for k in range(1, slab_count)]
        gathered, early_x = lax.optimization_barrier((gathered, early_x))
        queries, pairs, rest_piece = project(jnp.concatenate(gathered, axis=0), (own_q, own_pairs), piece_rows)

    def add_terms(held, sums, row_start=0, row_count=None):
        row_count = token_count if row_count is None else row_count
        return tuple(
            attend_block(queries, held, sums[0], sums[1], row_start, row_count, head_size, score_scale)
        )

    def add_masked(arrived, sums, row_start=0, row_count=None):
        for source, held in arrived:
            sums = lax.cond(
                allowed_from(source),
                lambda: add_terms(held, sums, row_start, row_count),
                lambda: sums,
            )
        return sums

    zeros = jnp.zeros((token_count, local_width), jnp.float32)
    from_x = early_x
    if slab_count > 1:
        from_x = jnp.concatenate([early_x, routed(rest_piece, across_x)], axis=1)
    first = round_one(pairs, from_x)
    sums = add_terms(pairs, (zeros, zeros))
    first, sums, w_pieces = lax.optimization_barrier((first, sums, w_pieces))
    second = round_two(first)
    sums = add_masked(first, sums)
    second, sums = lax.optimization_barrier((second, sums))
    last = round_three(second)
    sums = add_masked(second, sums)
    last, sums = lax.optimization_barrier((last, sums))

    att_pieces = [None] * slab_count
    for k in list(range(1, slab_count)) + [0]:
        row_start = k * piece_rows
        sums = add_masked(last, sums, row_start, piece_rows)
        rows = slice(row_start, row_start + piece_rows)
        attended = (sums[0][rows] / sums[1][rows]).astype(jnp.bfloat16)
        if k != 0:
            attended, last, sums = lax.optimization_barrier((attended, last, sums))
            attended = rotated(attended, "slab", -k)
        att_pieces[k] = attended
    mixed = jnp.dot(
        jnp.concatenate(att_pieces, axis=1),
        jnp.concatenate(w_pieces, axis=0),
        preferred_element_type=jnp.float32,
    )
    return mixed.astype(jnp.bfloat16)[None]


def solution(mesh):
    placed = (
        P("group", "slab", None),
        P(),
        P(None, None, "slab"),
        P(),
        P(),
        P("slab", None),
        P(),
        P(),
    )
    return jax.shard_map(
        body, mesh=mesh, in_specs=placed, out_specs=P("group", "slab", None), check_vma=False
    )
```

```python
import functools
import math

import jax
import jax.numpy as jnp
from jax import lax
from jax.sharding import PartitionSpec as P
from jax.experimental import pallas as pl
from jax.experimental.pallas import tpu as pltpu

REACH = 3


def shifted(block, axis, distance):
    devices = range(lax.axis_size(axis))
    route = [(i - distance, i) for i in devices if i - distance in devices]
    return lax.ppermute(block, axis, route)


def rotated(block, axis, distance):
    count = lax.axis_size(axis)
    route = [(i, (i + distance) % count) for i in range(count)]
    return lax.ppermute(block, axis, route)


def norm_rows(values, gain):
    centre = jnp.mean(values, axis=-1, keepdims=True)
    centred = values - centre
    spread = jnp.mean(centred * centred, axis=-1, keepdims=True)
    return centred * lax.rsqrt(spread + 1e-06) * gain


def block_terms(queries, key_rows, values, score_scale):
    scores = (
        jnp.einsum("qhd,khd->hqk", queries, key_rows, preferred_element_type=jnp.float32)
        * score_scale
    )
    weights = jnp.exp(scores).astype(jnp.bfloat16)
    numerator = jnp.einsum("hqk,khd->qhd", weights, values, preferred_element_type=jnp.float32)
    denominator = jnp.transpose(jnp.sum(weights, axis=2, dtype=jnp.float32))
    return (numerator, denominator)


def attention_kernel(q_ref, k_ref, v_ref, num_in, den_in, num_out, den_out, *, head_size, scale):
    queries = q_ref[...]
    keys = k_ref[...]
    values = v_ref[...]
    first = lax.broadcasted_iota(jnp.int32, (1, 2 * head_size), 1) < head_size
    parts = []
    for lanes in (first, jnp.logical_not(first)):
        head_keys = jnp.where(lanes, keys, jnp.zeros_like(keys))
        scores = lax.dot_general(
            queries, head_keys, (((1,), (1,)), ((), ())), preferred_element_type=jnp.float32
        )
        weights = jnp.exp(scores).astype(jnp.bfloat16)
        numerator = jnp.dot(weights, values, preferred_element_type=jnp.float32)
        denominator = jnp.sum(weights.astype(jnp.float32), axis=1, keepdims=True)
        parts.append((numerator, denominator))
    num_out[...] = num_in[...] + jnp.where(first, parts[0][0], parts[1][0])
    den_out[...] = den_in[...] + jnp.where(first, parts[0][1], parts[1][1])


def project_kernel(
    x_ref, w_ref, q_gain_ref, k_gain_ref, q_in, kv_in, q_ref, kv_ref, piece_ref, *, head_size, width, q_scale
):
    first = lax.broadcasted_iota(jnp.int32, (1, 2 * head_size), 1) < head_size

    def head_norm(values, gain):
        def head_mean(x):
            total_a = jnp.sum(jnp.where(first, x, 0.0), axis=1, keepdims=True)
            total_b = jnp.sum(jnp.where(first, 0.0, x), axis=1, keepdims=True)
            return jnp.where(first, total_a, total_b) / head_size

        centred = values - head_mean(values)
        spread = head_mean(centred * centred)
        return centred * lax.rsqrt(spread + 1e-06) * gain

    rows = x_ref[...]
    for part in range(3):
        projected = jnp.dot(
            rows, w_ref[part], preferred_element_type=jnp.float32
        )
        for pair in range(width // (2 * head_size)):
            lanes = slice(pair * 2 * head_size, (pair + 1) * 2 * head_size)
            if part == 0:
                rounded = head_norm(projected[:, lanes], q_gain_ref[...]).astype(q_ref.dtype)
                q_ref[:, lanes] = rounded * jnp.asarray(q_scale, q_ref.dtype)
            else:
                if part == 1:
                    block = head_norm(projected[:, lanes], k_gain_ref[...]).astype(kv_ref.dtype)
                else:
                    block = projected[:, lanes].astype(kv_ref.dtype)
                kv_ref[part - 1, :, lanes] = block
                piece_ref[part - 1, :, lanes] = block


def project_heads(rows, part_w, q_gain, k_gain, head_size, q_buf, kv_buf, row_start):
    assert math.log2(head_size) % 2 == 0
    row_count, full_width = rows.shape
    width = part_w.shape[2]
    tile = 256 if row_count % 256 == 0 else 128
    first_tile = row_start // tile
    pair_gain = lambda gain: jnp.tile(gain, 2).reshape(1, 2 * head_size)
    gain_spec = pl.BlockSpec((1, 2 * head_size), lambda i: (0, 0))
    q_spec = pl.BlockSpec((tile, width), lambda i: (i + first_tile, 0))
    kv_spec = pl.BlockSpec((2, tile, width), lambda i: (0, i + first_tile, 0))
    return pl.pallas_call(
        functools.partial(project_kernel, head_size=head_size, width=width, q_scale=head_size ** (-0.5)),
        grid=(row_count // tile,),
        in_specs=[
            pl.BlockSpec((tile, full_width), lambda i: (i, 0)),
            pl.BlockSpec((3, full_width, width), lambda i: (0, 0, 0)),
            gain_spec,
            gain_spec,
            q_spec,
            kv_spec,
        ],
        out_specs=[q_spec, kv_spec, pl.BlockSpec((2, tile, width), lambda i: (0, i, 0))],
        out_shape=[
            jax.ShapeDtypeStruct(q_buf.shape, jnp.bfloat16),
            jax.ShapeDtypeStruct(kv_buf.shape, jnp.bfloat16),
            jax.ShapeDtypeStruct((2, row_count, width), jnp.bfloat16),
        ],
        input_output_aliases={4: 0, 5: 1},
        cost_estimate=pl.CostEstimate(
            flops=2 * row_count * full_width * 3 * width,
            transcendentals=row_count * width,
            bytes_accessed=row_count * full_width * 2 + full_width * 6 * width + row_count * width * 6,
        ),
    )(rows, part_w, pair_gain(q_gain), pair_gain(k_gain), q_buf, kv_buf)


def attend_block(queries, held, numerator, denominator, row_start, row_count, head_size, scale):
    token_count, width = queries.shape
    key_count = held.shape[1]
    pair_width = 2 * head_size
    tile = min(row_count, 1024)
    first_tile = row_start // tile
    row_spec = pl.BlockSpec((tile, pair_width), lambda i, j: (i + first_tile, j))
    key_spec = pl.BlockSpec((None, key_count, pair_width), lambda i, j: (0, 0, j))
    value_spec = pl.BlockSpec((None, key_count, pair_width), lambda i, j: (1, 0, j))
    flops = 2 * 2 * 2 * row_count * key_count * width
    return pl.pallas_call(
        functools.partial(attention_kernel, head_size=head_size, scale=scale),
        grid=(row_count // tile, width // pair_width),
        in_specs=[row_spec, key_spec, value_spec, row_spec, row_spec],
        out_specs=[row_spec, row_spec],
        out_shape=[jax.ShapeDtypeStruct((token_count, width), jnp.float32)] * 2,
        input_output_aliases={3: 0, 4: 1},
        compiler_params=pltpu.CompilerParams(dimension_semantics=("arbitrary", "arbitrary")),
        cost_estimate=pl.CostEstimate(
            flops=flops,
            transcendentals=row_count * key_count * (width // head_size),
            bytes_accessed=row_count * width * 18 + key_count * width * 4 * (row_count // tile),
        ),
    )(queries, held, held, numerator, denominator)


def body(tokens, norm_gain, w_qkv, q_gain, k_gain, w_out, covis_mask, capture_rank):
    full_width = tokens.shape[2]
    local_width = w_qkv.shape[2]
    head_size = q_gain.shape[0]
    heads_here = local_width // head_size
    score_scale = head_size ** (-0.5)
    slab_count = lax.axis_size("slab")
    my_group = lax.axis_index("group")
    group_count = lax.axis_size("group")
    normed = norm_rows(tokens[0].astype(jnp.float32), norm_gain).astype(jnp.bfloat16)
    piece_rows = normed.shape[0]
    part_w = jnp.transpose(w_qkv, (1, 0, 2))

    token_count = tokens.shape[1] * slab_count

    def project(rows, buffers, row_start):
        return project_heads(rows, part_w, q_gain, k_gain, head_size, *buffers, row_start)

    empty = (
        jnp.zeros((token_count, local_width), jnp.bfloat16),
        jnp.zeros((2, token_count, local_width), jnp.bfloat16),
    )
    own_q, own_pairs, own_piece = project(normed, empty, 0)

    def allowed_from(source):
        in_range = (source >= 0) & (source < group_count)
        clipped = jnp.clip(source, 0, group_count - 1)
        return (
            in_range
            & (covis_mask[my_group, clipped] == 1)
            & (capture_rank[clipped] <= capture_rank[my_group])
        )

    def routed(block, route):
        return lax.ppermute(block, "group", [(a, b) for a, b in route if 0 <= b < group_count])

    g_all = range(group_count)
    spot = my_group % 4
    on_chip = [(g, g ^ 1) for g in g_all]
    across_x = [(g, g ^ 2) for g in g_all]
    along_z_once = [(g, g + 3) if g % 2 == 1 else (g, g - 3) for g in g_all]
    mixed_relay = [
        (g, g ^ 2) if g % 4 in (1, 2) else ((g, g + 5) if g % 4 == 0 else (g, g - 5)) for g in g_all
    ]

    def round_one(buf, from_x):
        return [
            (my_group ^ 1, routed(buf, on_chip)),
            (my_group ^ 2, from_x),
            (jnp.where(spot % 2 == 0, my_group - 3, my_group + 3), routed(buf, along_z_once)),
        ]

    def round_two(first):
        from_x, from_z = first[1][1], first[2][1]
        outgoing = jnp.where((spot == 1) | (spot == 2), from_z, from_x)
        source = jnp.where(
            spot == 0,
            my_group - 1,
            jnp.where(spot == 1, my_group - 3, jnp.where(spot == 2, my_group + 3, my_group + 1)),
        )
        return [
            (my_group ^ 3, routed(from_x, on_chip)),
            (source, routed(outgoing, mixed_relay)),
        ]

    def round_three(second):
        return [(jnp.where(spot < 2, my_group - 2, my_group + 2), routed(second[1][1], on_chip))]

    early_x = routed(own_piece, across_x)
    queries, pairs = own_q, own_pairs
    w_pieces = [w_out]
    if slab_count > 1:
        gathered = [rotated(normed, "slab", k) for k in range(1, slab_count)]
        w_later = lax.optimization_barrier((w_out, gathered))[0]
        w_pieces = w_pieces + [rotated(w_later, "slab", -k) for k in range(1, slab_count)]
        gathered, early_x = lax.optimization_barrier((gathered, early_x))
        queries, pairs, rest_piece = project(jnp.concatenate(gathered, axis=0), (own_q, own_pairs), piece_rows)

    def add_terms(held, sums, row_start=0, row_count=None):
        row_count = token_count if row_count is None else row_count
        return tuple(
            attend_block(queries, held, sums[0], sums[1], row_start, row_count, head_size, score_scale)
        )

    def add_masked(arrived, sums, row_start=0, row_count=None):
        for source, held in arrived:
            sums = lax.cond(
                allowed_from(source),
                lambda: add_terms(held, sums, row_start, row_count),
                lambda: sums,
            )
        return sums

    zeros = jnp.zeros((token_count, local_width), jnp.float32)
    from_x = early_x
    if slab_count > 1:
        from_x = jnp.concatenate([early_x, routed(rest_piece, across_x)], axis=1)
    first = round_one(pairs, from_x)
    sums = add_terms(pairs, (zeros, zeros))
    first, sums, w_pieces = lax.optimization_barrier((first, sums, w_pieces))
    second = round_two(first)
    sums = add_masked(first, sums)
    second, sums = lax.optimization_barrier((second, sums))
    last = round_three(second)
    sums = add_masked(second, sums)
    last, sums = lax.optimization_barrier((last, sums))

    att_pieces = [None] * slab_count
    for k in list(range(1, slab_count)) + [0]:
        row_start = k * piece_rows
        sums = add_masked(last, sums, row_start, piece_rows)
        rows = slice(row_start, row_start + piece_rows)
        attended = (sums[0][rows] / sums[1][rows]).astype(jnp.bfloat16)
        if k != 0:
            attended, last, sums = lax.optimization_barrier((attended, last, sums))
            attended = rotated(attended, "slab", -k)
        att_pieces[k] = attended
    mixed = jnp.dot(
        jnp.concatenate(att_pieces, axis=1),
        jnp.concatenate(w_pieces, axis=0),
        preferred_element_type=jnp.float32,
    )
    return mixed.astype(jnp.bfloat16)[None]


def solution(mesh):
    placed = (
        P("group", "slab", None),
        P(),
        P(None, None, "slab"),
        P(),
        P(),
        P("slab", None),
        P(),
        P(),
    )
    return jax.shard_map(
        body, mesh=mesh, in_specs=placed, out_specs=P("group", "slab", None), check_vma=False
    )
```

```python
import functools
import math

import jax
import jax.numpy as jnp
from jax import lax
from jax.sharding import PartitionSpec as P
from jax.experimental import pallas as pl
from jax.experimental.pallas import tpu as pltpu

REACH = 3


def shifted(block, axis, distance):
    devices = range(lax.axis_size(axis))
    route = [(i - distance, i) for i in devices if i - distance in devices]
    return lax.ppermute(block, axis, route)


def rotated(block, axis, distance):
    count = lax.axis_size(axis)
    route = [(i, (i + distance) % count) for i in range(count)]
    return lax.ppermute(block, axis, route)


def norm_rows(values, gain):
    centre = jnp.mean(values, axis=-1, keepdims=True)
    centred = values - centre
    spread = jnp.mean(centred * centred, axis=-1, keepdims=True)
    return centred * lax.rsqrt(spread + 1e-06) * gain


def block_terms(queries, key_rows, values, score_scale):
    scores = (
        jnp.einsum("qhd,khd->hqk", queries, key_rows, preferred_element_type=jnp.float32)
        * score_scale
    )
    weights = jnp.exp(scores).astype(jnp.bfloat16)
    numerator = jnp.einsum("hqk,khd->qhd", weights, values, preferred_element_type=jnp.float32)
    denominator = jnp.transpose(jnp.sum(weights, axis=2, dtype=jnp.float32))
    return (numerator, denominator)


def attention_kernel(q_ref, k_ref, v_ref, num_in, den_in, num_out, den_out, *, head_size, scale):
    queries = q_ref[...]
    keys = k_ref[...]
    values = v_ref[...]
    first = lax.broadcasted_iota(jnp.int32, (1, 2 * head_size), 1) < head_size
    ones = jnp.ones_like(values)
    parts = []
    for lanes in (first, jnp.logical_not(first)):
        head_keys = jnp.where(lanes, keys, jnp.zeros_like(keys))
        scores = lax.dot_general(
            queries, head_keys, (((1,), (1,)), ((), ())), preferred_element_type=jnp.float32
        )
        weights = jnp.exp(scores).astype(jnp.bfloat16)
        parts.append(jnp.dot(weights, jnp.where(lanes, values, ones), preferred_element_type=jnp.float32))
    num_out[...] = num_in[...] + jnp.where(first, parts[0], parts[1])
    den_out[...] = den_in[...] + jnp.where(first, parts[1], parts[0])


def project_kernel(
    x_ref, w_ref, q_gain_ref, k_gain_ref, q_in, kv_in, q_ref, kv_ref, piece_ref, *, head_size, width, q_scale
):
    first = lax.broadcasted_iota(jnp.int32, (1, 2 * head_size), 1) < head_size

    def head_norm(values, gain):
        def head_mean(x):
            total_a = jnp.sum(jnp.where(first, x, 0.0), axis=1, keepdims=True)
            total_b = jnp.sum(jnp.where(first, 0.0, x), axis=1, keepdims=True)
            return jnp.where(first, total_a, total_b) / head_size

        centred = values - head_mean(values)
        spread = head_mean(centred * centred)
        return centred * lax.rsqrt(spread + 1e-06) * gain

    rows = x_ref[...]
    for part in range(3):
        projected = jnp.dot(
            rows, w_ref[part], preferred_element_type=jnp.float32
        )
        for pair in range(width // (2 * head_size)):
            lanes = slice(pair * 2 * head_size, (pair + 1) * 2 * head_size)
            if part == 0:
                rounded = head_norm(projected[:, lanes], q_gain_ref[...]).astype(q_ref.dtype)
                q_ref[:, lanes] = rounded * jnp.asarray(q_scale, q_ref.dtype)
            else:
                if part == 1:
                    block = head_norm(projected[:, lanes], k_gain_ref[...]).astype(kv_ref.dtype)
                else:
                    block = projected[:, lanes].astype(kv_ref.dtype)
                kv_ref[part - 1, :, lanes] = block
                piece_ref[part - 1, :, lanes] = block


def project_heads(rows, part_w, q_gain, k_gain, head_size, q_buf, kv_buf, row_start):
    assert math.log2(head_size) % 2 == 0
    row_count, full_width = rows.shape
    width = part_w.shape[2]
    tile = 256 if row_count % 256 == 0 else 128
    first_tile = row_start // tile
    pair_gain = lambda gain: jnp.tile(gain, 2).reshape(1, 2 * head_size)
    gain_spec = pl.BlockSpec((1, 2 * head_size), lambda i: (0, 0))
    q_spec = pl.BlockSpec((tile, width), lambda i: (i + first_tile, 0))
    kv_spec = pl.BlockSpec((2, tile, width), lambda i: (0, i + first_tile, 0))
    return pl.pallas_call(
        functools.partial(project_kernel, head_size=head_size, width=width, q_scale=head_size ** (-0.5)),
        grid=(row_count // tile,),
        in_specs=[
            pl.BlockSpec((tile, full_width), lambda i: (i, 0)),
            pl.BlockSpec((3, full_width, width), lambda i: (0, 0, 0)),
            gain_spec,
            gain_spec,
            q_spec,
            kv_spec,
        ],
        out_specs=[q_spec, kv_spec, pl.BlockSpec((2, tile, width), lambda i: (0, i, 0))],
        out_shape=[
            jax.ShapeDtypeStruct(q_buf.shape, jnp.bfloat16),
            jax.ShapeDtypeStruct(kv_buf.shape, jnp.bfloat16),
            jax.ShapeDtypeStruct((2, row_count, width), jnp.bfloat16),
        ],
        input_output_aliases={4: 0, 5: 1},
        cost_estimate=pl.CostEstimate(
            flops=2 * row_count * full_width * 3 * width,
            transcendentals=row_count * width,
            bytes_accessed=row_count * full_width * 2 + full_width * 6 * width + row_count * width * 6,
        ),
    )(rows, part_w, pair_gain(q_gain), pair_gain(k_gain), q_buf, kv_buf)


def attend_block(queries, held, numerator, denominator, row_start, row_count, head_size, scale):
    token_count, width = queries.shape
    key_count = held.shape[1]
    pair_width = 2 * head_size
    tile = min(row_count, 1024)
    first_tile = row_start // tile
    row_spec = pl.BlockSpec((tile, pair_width), lambda i, j: (i + first_tile, j))
    key_spec = pl.BlockSpec((None, key_count, pair_width), lambda i, j: (0, 0, j))
    value_spec = pl.BlockSpec((None, key_count, pair_width), lambda i, j: (1, 0, j))
    flops = 2 * 2 * 2 * row_count * key_count * width
    return pl.pallas_call(
        functools.partial(attention_kernel, head_size=head_size, scale=scale),
        grid=(row_count // tile, width // pair_width),
        in_specs=[row_spec, key_spec, value_spec, row_spec, row_spec],
        out_specs=[row_spec, row_spec],
        out_shape=[jax.ShapeDtypeStruct((token_count, width), jnp.float32)] * 2,
        input_output_aliases={3: 0, 4: 1},
        compiler_params=pltpu.CompilerParams(dimension_semantics=("arbitrary", "arbitrary")),
        cost_estimate=pl.CostEstimate(
            flops=flops,
            transcendentals=row_count * key_count * (width // head_size),
            bytes_accessed=row_count * width * 18 + key_count * width * 4 * (row_count // tile),
        ),
    )(queries, held, held, numerator, denominator)


def body(tokens, norm_gain, w_qkv, q_gain, k_gain, w_out, covis_mask, capture_rank):
    full_width = tokens.shape[2]
    local_width = w_qkv.shape[2]
    head_size = q_gain.shape[0]
    heads_here = local_width // head_size
    score_scale = head_size ** (-0.5)
    slab_count = lax.axis_size("slab")
    my_group = lax.axis_index("group")
    group_count = lax.axis_size("group")
    normed = norm_rows(tokens[0].astype(jnp.float32), norm_gain).astype(jnp.bfloat16)
    piece_rows = normed.shape[0]
    part_w = jnp.transpose(w_qkv, (1, 0, 2))

    token_count = tokens.shape[1] * slab_count

    def project(rows, buffers, row_start):
        return project_heads(rows, part_w, q_gain, k_gain, head_size, *buffers, row_start)

    empty = (
        jnp.zeros((token_count, local_width), jnp.bfloat16),
        jnp.zeros((2, token_count, local_width), jnp.bfloat16),
    )
    own_q, own_pairs, own_piece = project(normed, empty, 0)

    def allowed_from(source):
        in_range = (source >= 0) & (source < group_count)
        clipped = jnp.clip(source, 0, group_count - 1)
        return (
            in_range
            & (covis_mask[my_group, clipped] == 1)
            & (capture_rank[clipped] <= capture_rank[my_group])
        )

    def routed(block, route):
        return lax.ppermute(block, "group", [(a, b) for a, b in route if 0 <= b < group_count])

    g_all = range(group_count)
    spot = my_group % 4
    on_chip = [(g, g ^ 1) for g in g_all]
    across_x = [(g, g ^ 2) for g in g_all]
    along_z_once = [(g, g + 3) if g % 2 == 1 else (g, g - 3) for g in g_all]
    mixed_relay = [
        (g, g ^ 2) if g % 4 in (1, 2) else ((g, g + 5) if g % 4 == 0 else (g, g - 5)) for g in g_all
    ]

    def round_one(buf, from_x):
        return [
            (my_group ^ 1, routed(buf, on_chip)),
            (my_group ^ 2, from_x),
            (jnp.where(spot % 2 == 0, my_group - 3, my_group + 3), routed(buf, along_z_once)),
        ]

    def round_two(first):
        from_x, from_z = first[1][1], first[2][1]
        outgoing = jnp.where((spot == 1) | (spot == 2), from_z, from_x)
        source = jnp.where(
            spot == 0,
            my_group - 1,
            jnp.where(spot == 1, my_group - 3, jnp.where(spot == 2, my_group + 3, my_group + 1)),
        )
        return [
            (my_group ^ 3, routed(from_x, on_chip)),
            (source, routed(outgoing, mixed_relay)),
        ]

    def round_three(second):
        return [(jnp.where(spot < 2, my_group - 2, my_group + 2), routed(second[1][1], on_chip))]

    early_x = routed(own_piece, across_x)
    queries, pairs = own_q, own_pairs
    w_pieces = [w_out]
    if slab_count > 1:
        gathered = [rotated(normed, "slab", k) for k in range(1, slab_count)]
        w_later = lax.optimization_barrier((w_out, gathered))[0]
        w_pieces = w_pieces + [rotated(w_later, "slab", -k) for k in range(1, slab_count)]
        gathered, early_x = lax.optimization_barrier((gathered, early_x))
        queries, pairs, rest_piece = project(jnp.concatenate(gathered, axis=0), (own_q, own_pairs), piece_rows)

    def add_terms(held, sums, row_start=0, row_count=None):
        row_count = token_count if row_count is None else row_count
        return tuple(
            attend_block(queries, held, sums[0], sums[1], row_start, row_count, head_size, score_scale)
        )

    def add_masked(arrived, sums, row_start=0, row_count=None):
        for source, held in arrived:
            sums = lax.cond(
                allowed_from(source),
                lambda: add_terms(held, sums, row_start, row_count),
                lambda: sums,
            )
        return sums

    zeros = jnp.zeros((token_count, local_width), jnp.float32)
    from_x = early_x
    if slab_count > 1:
        from_x = jnp.concatenate([early_x, routed(rest_piece, across_x)], axis=1)
    first = round_one(pairs, from_x)
    sums = add_terms(pairs, (zeros, zeros))
    first, sums, w_pieces = lax.optimization_barrier((first, sums, w_pieces))
    second = round_two(first)
    sums = add_masked(first, sums)
    second, sums = lax.optimization_barrier((second, sums))
    last = round_three(second)
    sums = add_masked(second, sums)
    last, sums = lax.optimization_barrier((last, sums))

    att_pieces = [None] * slab_count
    for k in list(range(1, slab_count)) + [0]:
        row_start = k * piece_rows
        sums = add_masked(last, sums, row_start, piece_rows)
        rows = slice(row_start, row_start + piece_rows)
        pair_count = local_width // (2 * head_size)
        swapped = sums[1][rows].reshape(piece_rows, pair_count, 2, head_size)
        denominator = jnp.flip(swapped, axis=2).reshape(piece_rows, local_width)
        attended = (sums[0][rows] / denominator).astype(jnp.bfloat16)
        if k != 0:
            attended, last, sums = lax.optimization_barrier((attended, last, sums))
            attended = rotated(attended, "slab", -k)
        att_pieces[k] = attended
    mixed = jnp.dot(
        jnp.concatenate(att_pieces, axis=1),
        jnp.concatenate(w_pieces, axis=0),
        preferred_element_type=jnp.float32,
    )
    return mixed.astype(jnp.bfloat16)[None]


def solution(mesh):
    placed = (
        P("group", "slab", None),
        P(),
        P(None, None, "slab"),
        P(),
        P(),
        P("slab", None),
        P(),
        P(),
    )
    return jax.shard_map(
        body, mesh=mesh, in_specs=placed, out_specs=P("group", "slab", None), check_vma=False
    )
```

```python
import functools
import math

import jax
import jax.numpy as jnp
from jax import lax
from jax.sharding import PartitionSpec as P
from jax.experimental import pallas as pl
from jax.experimental.pallas import tpu as pltpu

REACH = 3


def shifted(block, axis, distance):
    devices = range(lax.axis_size(axis))
    route = [(i - distance, i) for i in devices if i - distance in devices]
    return lax.ppermute(block, axis, route)


def rotated(block, axis, distance):
    count = lax.axis_size(axis)
    route = [(i, (i + distance) % count) for i in range(count)]
    return lax.ppermute(block, axis, route)


def norm_rows(values, gain):
    centre = jnp.mean(values, axis=-1, keepdims=True)
    centred = values - centre
    spread = jnp.mean(centred * centred, axis=-1, keepdims=True)
    return centred * lax.rsqrt(spread + 1e-06) * gain


def block_terms(queries, key_rows, values, score_scale):
    scores = (
        jnp.einsum("qhd,khd->hqk", queries, key_rows, preferred_element_type=jnp.float32)
        * score_scale
    )
    weights = jnp.exp(scores).astype(jnp.bfloat16)
    numerator = jnp.einsum("hqk,khd->qhd", weights, values, preferred_element_type=jnp.float32)
    denominator = jnp.transpose(jnp.sum(weights, axis=2, dtype=jnp.float32))
    return (numerator, denominator)


def attention_kernel(q_ref, k_ref, v_ref, num_in, den_in, num_out, den_out, *, head_size, scale):
    queries = q_ref[...]
    keys = k_ref[...]
    values = v_ref[...]
    first = lax.broadcasted_iota(jnp.int32, (1, 2 * head_size), 1) < head_size
    parts = []
    for lanes in (first, jnp.logical_not(first)):
        head_keys = jnp.where(lanes, keys, jnp.zeros_like(keys))
        scores = lax.dot_general(
            queries, head_keys, (((1,), (1,)), ((), ())), preferred_element_type=jnp.float32
        )
        weights = jnp.exp(scores).astype(jnp.bfloat16)
        numerator = jnp.dot(weights, values, preferred_element_type=jnp.float32)
        denominator = jnp.sum(weights.astype(jnp.float32), axis=1, keepdims=True)
        parts.append((numerator, denominator))
    num_out[...] = num_in[...] + jnp.where(first, parts[0][0], parts[1][0])
    den_out[...] = den_in[...] + jnp.where(first, parts[0][1], parts[1][1])


def project_kernel(
    x_ref, w_ref, q_gain_ref, k_gain_ref, q_in, kv_in, q_ref, kv_ref, piece_ref, *, head_size, width, q_scale
):
    first = lax.broadcasted_iota(jnp.int32, (1, 2 * head_size), 1) < head_size

    def head_norm(values, gain):
        def head_mean(x):
            total_a = jnp.sum(jnp.where(first, x, 0.0), axis=1, keepdims=True)
            total_b = jnp.sum(jnp.where(first, 0.0, x), axis=1, keepdims=True)
            return jnp.where(first, total_a, total_b) / head_size

        centred = values - head_mean(values)
        spread = head_mean(centred * centred)
        return centred * lax.rsqrt(spread + 1e-06) * gain

    rows = x_ref[...]
    for part in range(3):
        projected = jnp.dot(
            rows, w_ref[part], preferred_element_type=jnp.float32
        )
        for pair in range(width // (2 * head_size)):
            lanes = slice(pair * 2 * head_size, (pair + 1) * 2 * head_size)
            if part == 0:
                rounded = head_norm(projected[:, lanes], q_gain_ref[...]).astype(q_ref.dtype)
                q_ref[:, lanes] = rounded * jnp.asarray(q_scale, q_ref.dtype)
            else:
                if part == 1:
                    block = head_norm(projected[:, lanes], k_gain_ref[...]).astype(kv_ref.dtype)
                else:
                    block = projected[:, lanes].astype(kv_ref.dtype)
                kv_ref[part - 1, :, lanes] = block
                piece_ref[part - 1, :, lanes] = block


def project_heads(rows, part_w, q_gain, k_gain, head_size, q_buf, kv_buf, row_start):
    assert math.log2(head_size) % 2 == 0
    row_count, full_width = rows.shape
    width = part_w.shape[2]
    tile = 256 if row_count % 256 == 0 else 128
    first_tile = row_start // tile
    pair_gain = lambda gain: jnp.tile(gain, 2).reshape(1, 2 * head_size)
    gain_spec = pl.BlockSpec((1, 2 * head_size), lambda i: (0, 0))
    q_spec = pl.BlockSpec((tile, width), lambda i: (i + first_tile, 0))
    kv_spec = pl.BlockSpec((2, tile, width), lambda i: (0, i + first_tile, 0))
    return pl.pallas_call(
        functools.partial(project_kernel, head_size=head_size, width=width, q_scale=head_size ** (-0.5)),
        grid=(row_count // tile,),
        in_specs=[
            pl.BlockSpec((tile, full_width), lambda i: (i, 0)),
            pl.BlockSpec((3, full_width, width), lambda i: (0, 0, 0)),
            gain_spec,
            gain_spec,
            q_spec,
            kv_spec,
        ],
        out_specs=[q_spec, kv_spec, pl.BlockSpec((2, tile, width), lambda i: (0, i, 0))],
        out_shape=[
            jax.ShapeDtypeStruct(q_buf.shape, jnp.bfloat16),
            jax.ShapeDtypeStruct(kv_buf.shape, jnp.bfloat16),
            jax.ShapeDtypeStruct((2, row_count, width), jnp.bfloat16),
        ],
        input_output_aliases={4: 0, 5: 1},
        cost_estimate=pl.CostEstimate(
            flops=2 * row_count * full_width * 3 * width,
            transcendentals=row_count * width,
            bytes_accessed=row_count * full_width * 2 + full_width * 6 * width + row_count * width * 6,
        ),
    )(rows, part_w, pair_gain(q_gain), pair_gain(k_gain), q_buf, kv_buf)


def attend_block(queries, held, numerator, denominator, row_start, row_count, head_size, scale):
    token_count, width = queries.shape
    key_count = held.shape[1]
    pair_width = 2 * head_size
    tile = min(row_count, 1024)
    first_tile = row_start // tile
    row_spec = pl.BlockSpec((tile, pair_width), lambda i, j: (i + first_tile, j))
    key_spec = pl.BlockSpec((None, key_count, pair_width), lambda i, j: (0, 0, j))
    value_spec = pl.BlockSpec((None, key_count, pair_width), lambda i, j: (1, 0, j))
    flops = 2 * 2 * 2 * row_count * key_count * width
    return pl.pallas_call(
        functools.partial(attention_kernel, head_size=head_size, scale=scale),
        grid=(row_count // tile, width // pair_width),
        in_specs=[row_spec, key_spec, value_spec, row_spec, row_spec],
        out_specs=[row_spec, row_spec],
        out_shape=[jax.ShapeDtypeStruct((token_count, width), jnp.float32)] * 2,
        input_output_aliases={3: 0, 4: 1},
        compiler_params=pltpu.CompilerParams(dimension_semantics=("arbitrary", "arbitrary")),
        cost_estimate=pl.CostEstimate(
            flops=flops,
            transcendentals=row_count * key_count * (width // head_size),
            bytes_accessed=row_count * width * 18 + key_count * width * 4 * (row_count // tile),
        ),
    )(queries, held, held, numerator, denominator)


def body(tokens, norm_gain, w_qkv, q_gain, k_gain, w_out, covis_mask, capture_rank):
    full_width = tokens.shape[2]
    local_width = w_qkv.shape[2]
    head_size = q_gain.shape[0]
    heads_here = local_width // head_size
    score_scale = head_size ** (-0.5)
    slab_count = lax.axis_size("slab")
    my_group = lax.axis_index("group")
    group_count = lax.axis_size("group")
    normed = norm_rows(tokens[0].astype(jnp.float32), norm_gain).astype(jnp.bfloat16)
    piece_rows = normed.shape[0]
    part_w = jnp.transpose(w_qkv, (1, 0, 2))

    token_count = tokens.shape[1] * slab_count

    def project(rows, buffers, row_start):
        return project_heads(rows, part_w, q_gain, k_gain, head_size, *buffers, row_start)

    empty = (
        jnp.zeros((token_count, local_width), jnp.bfloat16),
        jnp.zeros((2, token_count, local_width), jnp.bfloat16),
    )
    own_q, own_pairs, own_piece = project(normed, empty, 0)

    def allowed_from(source):
        in_range = (source >= 0) & (source < group_count)
        clipped = jnp.clip(source, 0, group_count - 1)
        return (
            in_range
            & (covis_mask[my_group, clipped] == 1)
            & (capture_rank[clipped] <= capture_rank[my_group])
        )

    def routed(block, route):
        return lax.ppermute(block, "group", [(a, b) for a, b in route if 0 <= b < group_count])

    g_all = range(group_count)
    spot = my_group % 4
    on_chip = [(g, g ^ 1) for g in g_all]
    across_x = [(g, g ^ 2) for g in g_all]
    along_z_once = [(g, g + 3) if g % 2 == 1 else (g, g - 3) for g in g_all]
    mixed_relay = [
        (g, g ^ 2) if g % 4 in (1, 2) else ((g, g + 5) if g % 4 == 0 else (g, g - 5)) for g in g_all
    ]

    def round_one(buf, from_x):
        return [
            (my_group ^ 1, routed(buf, on_chip)),
            (my_group ^ 2, from_x),
            (jnp.where(spot % 2 == 0, my_group - 3, my_group + 3), routed(buf, along_z_once)),
        ]

    def round_two(first):
        from_x, from_z = first[1][1], first[2][1]
        outgoing = jnp.where((spot == 1) | (spot == 2), from_z, from_x)
        source = jnp.where(
            spot == 0,
            my_group - 1,
            jnp.where(spot == 1, my_group - 3, jnp.where(spot == 2, my_group + 3, my_group + 1)),
        )
        return [
            (my_group ^ 3, routed(from_x, on_chip)),
            (source, routed(outgoing, mixed_relay)),
        ]

    def round_three(second):
        return [(jnp.where(spot < 2, my_group - 2, my_group + 2), routed(second[1][1], on_chip))]

    early_x = routed(own_piece, across_x)
    queries, pairs = own_q, own_pairs
    w_pieces = [w_out]
    if slab_count > 1:
        gathered = [rotated(normed, "slab", k) for k in range(1, slab_count)]
        w_later = lax.optimization_barrier((w_out, gathered))[0]
        w_pieces = w_pieces + [rotated(w_later, "slab", -k) for k in range(1, slab_count)]
        gathered, early_x = lax.optimization_barrier((gathered, early_x))
        queries, pairs, rest_piece = project(jnp.concatenate(gathered, axis=0), (own_q, own_pairs), piece_rows)

    def add_terms(held, sums, row_start=0, row_count=None):
        row_count = token_count if row_count is None else row_count
        return tuple(
            attend_block(queries, held, sums[0], sums[1], row_start, row_count, head_size, score_scale)
        )

    def add_masked(arrived, sums, row_start=0, row_count=None):
        for source, held in arrived:
            sums = lax.cond(
                allowed_from(source),
                lambda: add_terms(held, sums, row_start, row_count),
                lambda: sums,
            )
        return sums

    zeros = jnp.zeros((token_count, local_width), jnp.float32)
    from_x = early_x
    if slab_count > 1:
        from_x = jnp.concatenate([early_x, routed(rest_piece, across_x)], axis=1)
    first = round_one(pairs, from_x)
    sums = add_terms(pairs, (zeros, zeros))
    near, sums = lax.optimization_barrier((first[:1], sums))
    sums = add_masked(near, sums)
    far, sums, w_pieces = lax.optimization_barrier((first[1:], sums, w_pieces))
    first = near + far
    second = round_two(first)
    sums = add_masked(far, sums)
    second, sums = lax.optimization_barrier((second, sums))
    last = round_three(second)
    sums = add_masked(second, sums)
    last, sums = lax.optimization_barrier((last, sums))

    att_pieces = [None] * slab_count
    for k in list(range(1, slab_count)) + [0]:
        row_start = k * piece_rows
        sums = add_masked(last, sums, row_start, piece_rows)
        rows = slice(row_start, row_start + piece_rows)
        attended = (sums[0][rows] / sums[1][rows]).astype(jnp.bfloat16)
        if k != 0:
            attended, last, sums = lax.optimization_barrier((attended, last, sums))
            attended = rotated(attended, "slab", -k)
        att_pieces[k] = attended
    mixed = jnp.dot(
        jnp.concatenate(att_pieces, axis=1),
        jnp.concatenate(w_pieces, axis=0),
        preferred_element_type=jnp.float32,
    )
    return mixed.astype(jnp.bfloat16)[None]


def solution(mesh):
    placed = (
        P("group", "slab", None),
        P(),
        P(None, None, "slab"),
        P(),
        P(),
        P("slab", None),
        P(),
        P(),
    )
    return jax.shard_map(
        body, mesh=mesh, in_specs=placed, out_specs=P("group", "slab", None), check_vma=False
    )
```

```python
import functools
import math

import jax
import jax.numpy as jnp
from jax import lax
from jax.sharding import PartitionSpec as P
from jax.experimental import pallas as pl
from jax.experimental.pallas import tpu as pltpu

REACH = 3


def shifted(block, axis, distance):
    devices = range(lax.axis_size(axis))
    route = [(i - distance, i) for i in devices if i - distance in devices]
    return lax.ppermute(block, axis, route)


def rotated(block, axis, distance):
    count = lax.axis_size(axis)
    route = [(i, (i + distance) % count) for i in range(count)]
    return lax.ppermute(block, axis, route)


def norm_rows(values, gain):
    centre = jnp.mean(values, axis=-1, keepdims=True)
    centred = values - centre
    spread = jnp.mean(centred * centred, axis=-1, keepdims=True)
    return centred * lax.rsqrt(spread + 1e-06) * gain


def block_terms(queries, key_rows, values, score_scale):
    scores = (
        jnp.einsum("qhd,khd->hqk", queries, key_rows, preferred_element_type=jnp.float32)
        * score_scale
    )
    weights = jnp.exp(scores).astype(jnp.bfloat16)
    numerator = jnp.einsum("hqk,khd->qhd", weights, values, preferred_element_type=jnp.float32)
    denominator = jnp.transpose(jnp.sum(weights, axis=2, dtype=jnp.float32))
    return (numerator, denominator)


def attention_kernel(q_ref, k_ref, v_ref, num_in, den_in, num_out, den_out, *, head_size, scale):
    queries = q_ref[...]
    keys = k_ref[...]
    values = v_ref[...]
    first = lax.broadcasted_iota(jnp.int32, (1, 2 * head_size), 1) < head_size
    parts = []
    for lanes in (first, jnp.logical_not(first)):
        head_keys = jnp.where(lanes, keys, jnp.zeros_like(keys))
        scores = lax.dot_general(
            queries, head_keys, (((1,), (1,)), ((), ())), preferred_element_type=jnp.float32
        )
        weights = jnp.exp(scores).astype(jnp.bfloat16)
        numerator = jnp.dot(weights, values, preferred_element_type=jnp.float32)
        denominator = jnp.sum(weights.astype(jnp.float32), axis=1, keepdims=True)
        parts.append((numerator, denominator))
    num_out[...] = num_in[...] + jnp.where(first, parts[0][0], parts[1][0])
    den_out[...] = den_in[...] + jnp.where(first, parts[0][1], parts[1][1])


def project_kernel(
    x_ref, w_ref, q_gain_ref, k_gain_ref, q_in, kv_in, q_ref, kv_ref, piece_ref, *, head_size, width, q_scale
):
    first = lax.broadcasted_iota(jnp.int32, (1, 2 * head_size), 1) < head_size

    def head_norm(values, gain):
        def head_mean(x):
            total_a = jnp.sum(jnp.where(first, x, 0.0), axis=1, keepdims=True)
            total_b = jnp.sum(jnp.where(first, 0.0, x), axis=1, keepdims=True)
            return jnp.where(first, total_a, total_b) / head_size

        centred = values - head_mean(values)
        spread = head_mean(centred * centred)
        return centred * lax.rsqrt(spread + 1e-06) * gain

    rows = x_ref[...]
    for part in range(3):
        projected = jnp.dot(
            rows, w_ref[part], preferred_element_type=jnp.float32
        )
        for pair in range(width // (2 * head_size)):
            lanes = slice(pair * 2 * head_size, (pair + 1) * 2 * head_size)
            if part == 0:
                rounded = head_norm(projected[:, lanes], q_gain_ref[...]).astype(q_ref.dtype)
                q_ref[:, lanes] = rounded * jnp.asarray(q_scale, q_ref.dtype)
            else:
                if part == 1:
                    block = head_norm(projected[:, lanes], k_gain_ref[...]).astype(kv_ref.dtype)
                else:
                    block = projected[:, lanes].astype(kv_ref.dtype)
                kv_ref[part - 1, :, lanes] = block
                piece_ref[part - 1, :, lanes] = block


def project_heads(rows, part_w, q_gain, k_gain, head_size, q_buf, kv_buf, row_start):
    assert math.log2(head_size) % 2 == 0
    row_count, full_width = rows.shape
    width = part_w.shape[2]
    tile = 256 if row_count % 256 == 0 else 128
    first_tile = row_start // tile
    pair_gain = lambda gain: jnp.tile(gain, 2).reshape(1, 2 * head_size)
    gain_spec = pl.BlockSpec((1, 2 * head_size), lambda i: (0, 0))
    q_spec = pl.BlockSpec((tile, width), lambda i: (i + first_tile, 0))
    kv_spec = pl.BlockSpec((2, tile, width), lambda i: (0, i + first_tile, 0))
    return pl.pallas_call(
        functools.partial(project_kernel, head_size=head_size, width=width, q_scale=head_size ** (-0.5)),
        grid=(row_count // tile,),
        in_specs=[
            pl.BlockSpec((tile, full_width), lambda i: (i, 0)),
            pl.BlockSpec((3, full_width, width), lambda i: (0, 0, 0)),
            gain_spec,
            gain_spec,
            q_spec,
            kv_spec,
        ],
        out_specs=[q_spec, kv_spec, pl.BlockSpec((2, tile, width), lambda i: (0, i, 0))],
        out_shape=[
            jax.ShapeDtypeStruct(q_buf.shape, jnp.bfloat16),
            jax.ShapeDtypeStruct(kv_buf.shape, jnp.bfloat16),
            jax.ShapeDtypeStruct((2, row_count, width), jnp.bfloat16),
        ],
        input_output_aliases={4: 0, 5: 1},
        cost_estimate=pl.CostEstimate(
            flops=2 * row_count * full_width * 3 * width,
            transcendentals=row_count * width,
            bytes_accessed=row_count * full_width * 2 + full_width * 6 * width + row_count * width * 6,
        ),
    )(rows, part_w, pair_gain(q_gain), pair_gain(k_gain), q_buf, kv_buf)


def attend_block(queries, held, numerator, denominator, row_start, row_count, head_size, scale):
    token_count, width = queries.shape
    key_count = held.shape[1]
    pair_width = 2 * head_size
    tile = min(row_count, 1024)
    first_tile = row_start // tile
    row_spec = pl.BlockSpec((tile, pair_width), lambda i, j: (i + first_tile, j))
    key_spec = pl.BlockSpec((None, key_count, pair_width), lambda i, j: (0, 0, j))
    value_spec = pl.BlockSpec((None, key_count, pair_width), lambda i, j: (1, 0, j))
    flops = 2 * 2 * 2 * row_count * key_count * width
    return pl.pallas_call(
        functools.partial(attention_kernel, head_size=head_size, scale=scale),
        grid=(row_count // tile, width // pair_width),
        in_specs=[row_spec, key_spec, value_spec, row_spec, row_spec],
        out_specs=[row_spec, row_spec],
        out_shape=[jax.ShapeDtypeStruct((token_count, width), jnp.float32)] * 2,
        input_output_aliases={3: 0, 4: 1},
        compiler_params=pltpu.CompilerParams(dimension_semantics=("arbitrary", "arbitrary")),
        cost_estimate=pl.CostEstimate(
            flops=flops,
            transcendentals=row_count * key_count * (width // head_size),
            bytes_accessed=row_count * width * 18 + key_count * width * 4 * (row_count // tile),
        ),
    )(queries, held, held, numerator, denominator)


def body(tokens, norm_gain, w_qkv, q_gain, k_gain, w_out, covis_mask, capture_rank):
    full_width = tokens.shape[2]
    local_width = w_qkv.shape[2]
    head_size = q_gain.shape[0]
    heads_here = local_width // head_size
    score_scale = head_size ** (-0.5)
    slab_count = lax.axis_size("slab")
    my_group = lax.axis_index("group")
    group_count = lax.axis_size("group")
    normed = norm_rows(tokens[0].astype(jnp.float32), norm_gain).astype(jnp.bfloat16)
    piece_rows = normed.shape[0]
    part_w = jnp.transpose(w_qkv, (1, 0, 2))

    token_count = tokens.shape[1] * slab_count

    def project(rows, buffers, row_start):
        return project_heads(rows, part_w, q_gain, k_gain, head_size, *buffers, row_start)

    empty = (
        jnp.zeros((token_count, local_width), jnp.bfloat16),
        jnp.zeros((2, token_count, local_width), jnp.bfloat16),
    )
    own_q, own_pairs, own_piece = project(normed, empty, 0)

    def allowed_from(source):
        in_range = (source >= 0) & (source < group_count)
        clipped = jnp.clip(source, 0, group_count - 1)
        return (
            in_range
            & (covis_mask[my_group, clipped] == 1)
            & (capture_rank[clipped] <= capture_rank[my_group])
        )

    def routed(block, route):
        return lax.ppermute(block, "group", [(a, b) for a, b in route if 0 <= b < group_count])

    g_all = range(group_count)
    spot = my_group % 4
    on_chip = [(g, g ^ 1) for g in g_all]
    across_x = [(g, g ^ 2) for g in g_all]
    along_z_once = [(g, g + 3) if g % 2 == 1 else (g, g - 3) for g in g_all]
    mixed_relay = [
        (g, g ^ 2) if g % 4 in (1, 2) else ((g, g + 5) if g % 4 == 0 else (g, g - 5)) for g in g_all
    ]

    def round_one(buf, from_x):
        return [
            (my_group ^ 1, routed(buf, on_chip)),
            (my_group ^ 2, from_x),
            (jnp.where(spot % 2 == 0, my_group - 3, my_group + 3), routed(buf, along_z_once)),
        ]

    def round_two(first):
        from_x, from_z = first[1][1], first[2][1]
        outgoing = jnp.where((spot == 1) | (spot == 2), from_z, from_x)
        source = jnp.where(
            spot == 0,
            my_group - 1,
            jnp.where(spot == 1, my_group - 3, jnp.where(spot == 2, my_group + 3, my_group + 1)),
        )
        return [
            (my_group ^ 3, routed(from_x, on_chip)),
            (source, routed(outgoing, mixed_relay)),
        ]

    def round_three(second):
        return [(jnp.where(spot < 2, my_group - 2, my_group + 2), routed(second[1][1], on_chip))]

    early_x = routed(own_piece, across_x)
    queries, pairs = own_q, own_pairs
    w_pieces = [w_out]
    if slab_count > 1:
        gathered = [rotated(normed, "slab", k) for k in range(1, slab_count)]
        w_later = lax.optimization_barrier((w_out, gathered))[0]
        w_pieces = w_pieces + [rotated(w_later, "slab", -k) for k in range(1, slab_count)]
        gathered, early_x = lax.optimization_barrier((gathered, early_x))
        queries, pairs, rest_piece = project(jnp.concatenate(gathered, axis=0), (own_q, own_pairs), piece_rows)

    def add_terms(held, sums, row_start=0, row_count=None):
        row_count = token_count if row_count is None else row_count
        return tuple(
            attend_block(queries, held, sums[0], sums[1], row_start, row_count, head_size, score_scale)
        )

    def add_masked(arrived, sums, row_start=0, row_count=None):
        for source, held in arrived:
            sums = lax.cond(
                allowed_from(source),
                lambda: add_terms(held, sums, row_start, row_count),
                lambda: sums,
            )
        return sums

    zeros = jnp.zeros((token_count, local_width), jnp.float32)
    from_x = early_x
    if slab_count > 1:
        from_x = jnp.concatenate([early_x, routed(rest_piece, across_x)], axis=1)
    first = round_one(pairs, from_x)
    sums = add_terms(pairs, (zeros, zeros))
    first, sums, w_pieces = lax.optimization_barrier((first, sums, w_pieces))
    second = round_two(first)
    sums = add_masked(first, sums)
    second, sums = lax.optimization_barrier((second, sums))
    last = round_three(second)
    sums = add_masked(second, sums)
    last, sums = lax.optimization_barrier((last, sums))

    att_pieces = [None] * slab_count
    for k in list(range(1, slab_count)) + [0]:
        row_start = k * piece_rows
        sums = add_masked(last, sums, row_start, piece_rows)
        rows = slice(row_start, row_start + piece_rows)
        attended = (sums[0][rows] / sums[1][rows]).astype(jnp.bfloat16)
        if k != 0:
            attended, last, sums = lax.optimization_barrier((attended, last, sums))
            attended = rotated(attended, "slab", -k)
        att_pieces[k] = attended
    mixed = jnp.dot(att_pieces[0], w_pieces[0], preferred_element_type=jnp.float32)
    if slab_count > 1:
        arrived, mixed = lax.optimization_barrier((att_pieces[1:], mixed))
        mixed = mixed + jnp.dot(
            jnp.concatenate(arrived, axis=1),
            jnp.concatenate(w_pieces[1:], axis=0),
            preferred_element_type=jnp.float32,
        )
    return mixed.astype(jnp.bfloat16)[None]


def solution(mesh):
    placed = (
        P("group", "slab", None),
        P(),
        P(None, None, "slab"),
        P(),
        P(),
        P("slab", None),
        P(),
        P(),
    )
    return jax.shard_map(
        body, mesh=mesh, in_specs=placed, out_specs=P("group", "slab", None), check_vma=False
    )
```

```python
import functools
import math

import jax
import jax.numpy as jnp
from jax import lax
from jax.sharding import PartitionSpec as P
from jax.experimental import pallas as pl
from jax.experimental.pallas import tpu as pltpu

REACH = 3


def shifted(block, axis, distance):
    devices = range(lax.axis_size(axis))
    route = [(i - distance, i) for i in devices if i - distance in devices]
    return lax.ppermute(block, axis, route)


def rotated(block, axis, distance):
    count = lax.axis_size(axis)
    route = [(i, (i + distance) % count) for i in range(count)]
    return lax.ppermute(block, axis, route)


def norm_rows(values, gain):
    centre = jnp.mean(values, axis=-1, keepdims=True)
    centred = values - centre
    spread = jnp.mean(centred * centred, axis=-1, keepdims=True)
    return centred * lax.rsqrt(spread + 1e-06) * gain


def block_terms(queries, key_rows, values, score_scale):
    scores = (
        jnp.einsum("qhd,khd->hqk", queries, key_rows, preferred_element_type=jnp.float32)
        * score_scale
    )
    weights = jnp.exp(scores).astype(jnp.bfloat16)
    numerator = jnp.einsum("hqk,khd->qhd", weights, values, preferred_element_type=jnp.float32)
    denominator = jnp.transpose(jnp.sum(weights, axis=2, dtype=jnp.float32))
    return (numerator, denominator)


def attention_kernel(q_ref, k_ref, v_ref, num_in, den_in, num_out, den_out, *, head_size, scale):
    queries = q_ref[...]
    keys = k_ref[...]
    values = v_ref[...]
    first = lax.broadcasted_iota(jnp.int32, (1, 2 * head_size), 1) < head_size
    parts = []
    for lanes in (first, jnp.logical_not(first)):
        head_keys = jnp.where(lanes, keys, jnp.zeros_like(keys))
        scores = lax.dot_general(
            queries, head_keys, (((1,), (1,)), ((), ())), preferred_element_type=jnp.float32
        )
        weights = jnp.exp(scores).astype(jnp.bfloat16)
        numerator = jnp.dot(weights, values, preferred_element_type=jnp.float32)
        denominator = jnp.sum(weights.astype(jnp.float32), axis=1, keepdims=True)
        parts.append((numerator, denominator))
    num_out[...] = num_in[...] + jnp.where(first, parts[0][0], parts[1][0])
    den_out[...] = den_in[...] + jnp.where(first, parts[0][1], parts[1][1])


def project_kernel(
    x_ref, w_ref, q_gain_ref, k_gain_ref, q_in, kv_in, q_ref, kv_ref, piece_ref, *, head_size, width, q_scale
):
    first = lax.broadcasted_iota(jnp.int32, (1, 2 * head_size), 1) < head_size

    def head_norm(values, gain):
        def head_mean(x):
            total_a = jnp.sum(jnp.where(first, x, 0.0), axis=1, keepdims=True)
            total_b = jnp.sum(jnp.where(first, 0.0, x), axis=1, keepdims=True)
            return jnp.where(first, total_a, total_b) / head_size

        centred = values - head_mean(values)
        spread = head_mean(centred * centred)
        return centred * lax.rsqrt(spread + 1e-06) * gain

    rows = x_ref[...]
    for part in range(3):
        projected = jnp.dot(
            rows, w_ref[part], preferred_element_type=jnp.float32
        )
        for pair in range(width // (2 * head_size)):
            lanes = slice(pair * 2 * head_size, (pair + 1) * 2 * head_size)
            if part == 0:
                rounded = head_norm(projected[:, lanes], q_gain_ref[...]).astype(q_ref.dtype)
                q_ref[:, lanes] = rounded * jnp.asarray(q_scale, q_ref.dtype)
            else:
                if part == 1:
                    block = head_norm(projected[:, lanes], k_gain_ref[...]).astype(kv_ref.dtype)
                else:
                    block = projected[:, lanes].astype(kv_ref.dtype)
                kv_ref[part - 1, :, lanes] = block
                piece_ref[part - 1, :, lanes] = block


def project_heads(rows, part_w, q_gain, k_gain, head_size, q_buf, kv_buf, row_start):
    assert math.log2(head_size) % 2 == 0
    row_count, full_width = rows.shape
    width = part_w.shape[2]
    tile = 256 if row_count % 256 == 0 else 128
    first_tile = row_start // tile
    pair_gain = lambda gain: jnp.tile(gain, 2).reshape(1, 2 * head_size)
    gain_spec = pl.BlockSpec((1, 2 * head_size), lambda i: (0, 0))
    q_spec = pl.BlockSpec((tile, width), lambda i: (i + first_tile, 0))
    kv_spec = pl.BlockSpec((2, tile, width), lambda i: (0, i + first_tile, 0))
    return pl.pallas_call(
        functools.partial(project_kernel, head_size=head_size, width=width, q_scale=head_size ** (-0.5)),
        grid=(row_count // tile,),
        in_specs=[
            pl.BlockSpec((tile, full_width), lambda i: (i, 0)),
            pl.BlockSpec((3, full_width, width), lambda i: (0, 0, 0)),
            gain_spec,
            gain_spec,
            q_spec,
            kv_spec,
        ],
        out_specs=[q_spec, kv_spec, pl.BlockSpec((2, tile, width), lambda i: (0, i, 0))],
        out_shape=[
            jax.ShapeDtypeStruct(q_buf.shape, jnp.bfloat16),
            jax.ShapeDtypeStruct(kv_buf.shape, jnp.bfloat16),
            jax.ShapeDtypeStruct((2, row_count, width), jnp.bfloat16),
        ],
        input_output_aliases={4: 0, 5: 1},
        cost_estimate=pl.CostEstimate(
            flops=2 * row_count * full_width * 3 * width,
            transcendentals=row_count * width,
            bytes_accessed=row_count * full_width * 2 + full_width * 6 * width + row_count * width * 6,
        ),
    )(rows, part_w, pair_gain(q_gain), pair_gain(k_gain), q_buf, kv_buf)


def attend_block(queries, held, numerator, denominator, row_start, row_count, head_size, scale):
    token_count, width = queries.shape
    key_count = held.shape[1]
    pair_width = 2 * head_size
    tile = min(row_count, 1024)
    first_tile = row_start // tile
    row_spec = pl.BlockSpec((tile, pair_width), lambda i, j: (i + first_tile, j))
    key_spec = pl.BlockSpec((None, key_count, pair_width), lambda i, j: (0, 0, j))
    value_spec = pl.BlockSpec((None, key_count, pair_width), lambda i, j: (1, 0, j))
    flops = 2 * 2 * 2 * row_count * key_count * width
    return pl.pallas_call(
        functools.partial(attention_kernel, head_size=head_size, scale=scale),
        grid=(row_count // tile, width // pair_width),
        in_specs=[row_spec, key_spec, value_spec, row_spec, row_spec],
        out_specs=[row_spec, row_spec],
        out_shape=[jax.ShapeDtypeStruct((token_count, width), jnp.float32)] * 2,
        input_output_aliases={3: 0, 4: 1},
        compiler_params=pltpu.CompilerParams(dimension_semantics=("arbitrary", "arbitrary")),
        cost_estimate=pl.CostEstimate(
            flops=flops,
            transcendentals=row_count * key_count * (width // head_size),
            bytes_accessed=row_count * width * 18 + key_count * width * 4 * (row_count // tile),
        ),
    )(queries, held, held, numerator, denominator)


def body(tokens, norm_gain, w_qkv, q_gain, k_gain, w_out, covis_mask, capture_rank):
    full_width = tokens.shape[2]
    local_width = w_qkv.shape[2]
    head_size = q_gain.shape[0]
    heads_here = local_width // head_size
    score_scale = head_size ** (-0.5)
    slab_count = lax.axis_size("slab")
    my_group = lax.axis_index("group")
    group_count = lax.axis_size("group")
    normed = norm_rows(tokens[0].astype(jnp.float32), norm_gain).astype(jnp.bfloat16)
    piece_rows = normed.shape[0]
    part_w = jnp.transpose(w_qkv, (1, 0, 2))

    token_count = tokens.shape[1] * slab_count

    def project(rows, buffers, row_start):
        return project_heads(rows, part_w, q_gain, k_gain, head_size, *buffers, row_start)

    empty = (
        jnp.zeros((token_count, local_width), jnp.bfloat16),
        jnp.zeros((2, token_count, local_width), jnp.bfloat16),
    )
    own_q, own_pairs, own_piece = project(normed, empty, 0)

    def allowed_from(source):
        in_range = (source >= 0) & (source < group_count)
        clipped = jnp.clip(source, 0, group_count - 1)
        return (
            in_range
            & (covis_mask[my_group, clipped] == 1)
            & (capture_rank[clipped] <= capture_rank[my_group])
        )

    def routed(block, route):
        return lax.ppermute(block, "group", [(a, b) for a, b in route if 0 <= b < group_count])

    g_all = range(group_count)
    spot = my_group % 4
    on_chip = [(g, g ^ 1) for g in g_all]
    across_x = [(g, g ^ 2) for g in g_all]
    along_z_once = [(g, g + 3) if g % 2 == 1 else (g, g - 3) for g in g_all]
    mixed_relay = [
        (g, g ^ 2) if g % 4 in (1, 2) else ((g, g + 5) if g % 4 == 0 else (g, g - 5)) for g in g_all
    ]

    def round_one(buf, from_x):
        return [
            (my_group ^ 1, routed(buf, on_chip)),
            (my_group ^ 2, from_x),
            (jnp.where(spot % 2 == 0, my_group - 3, my_group + 3), routed(buf, along_z_once)),
        ]

    def round_two(first):
        from_x, from_z = first[1][1], first[2][1]
        outgoing = jnp.where((spot == 1) | (spot == 2), from_z, from_x)
        source = jnp.where(
            spot == 0,
            my_group - 1,
            jnp.where(spot == 1, my_group - 3, jnp.where(spot == 2, my_group + 3, my_group + 1)),
        )
        return [
            (my_group ^ 3, routed(from_x, on_chip)),
            (source, routed(outgoing, mixed_relay)),
        ]

    def round_three(second):
        return [(jnp.where(spot < 2, my_group - 2, my_group + 2), routed(second[1][1], on_chip))]

    queries, pairs = own_q, own_pairs
    w_pieces = [w_out]
    if slab_count > 1:
        gathered = [rotated(normed, "slab", k) for k in range(1, slab_count)]
        w_later = lax.optimization_barrier((w_out, gathered))[0]
        w_pieces = w_pieces + [rotated(w_later, "slab", -k) for k in range(1, slab_count)]
        queries, pairs, rest_piece = project(jnp.concatenate(gathered, axis=0), (own_q, own_pairs), piece_rows)

    def add_terms(held, sums, row_start=0, row_count=None):
        row_count = token_count if row_count is None else row_count
        return tuple(
            attend_block(queries, held, sums[0], sums[1], row_start, row_count, head_size, score_scale)
        )

    def add_masked(arrived, sums, row_start=0, row_count=None):
        for source, held in arrived:
            sums = lax.cond(
                allowed_from(source),
                lambda: add_terms(held, sums, row_start, row_count),
                lambda: sums,
            )
        return sums

    zeros = jnp.zeros((token_count, local_width), jnp.float32)
    first = round_one(pairs, routed(pairs, across_x))
    sums = add_terms(pairs, (zeros, zeros))
    first, sums, w_pieces = lax.optimization_barrier((first, sums, w_pieces))
    second = round_two(first)
    sums = add_masked(first, sums)
    second, sums = lax.optimization_barrier((second, sums))
    last = round_three(second)
    sums = add_masked(second, sums)
    last, sums = lax.optimization_barrier((last, sums))

    att_pieces = [None] * slab_count
    for k in list(range(1, slab_count)) + [0]:
        row_start = k * piece_rows
        sums = add_masked(last, sums, row_start, piece_rows)
        rows = slice(row_start, row_start + piece_rows)
        attended = (sums[0][rows] / sums[1][rows]).astype(jnp.bfloat16)
        if k != 0:
            attended, last, sums = lax.optimization_barrier((attended, last, sums))
            attended = rotated(attended, "slab", -k)
        att_pieces[k] = attended
    mixed = jnp.dot(
        jnp.concatenate(att_pieces, axis=1),
        jnp.concatenate(w_pieces, axis=0),
        preferred_element_type=jnp.float32,
    )
    return mixed.astype(jnp.bfloat16)[None]


def solution(mesh):
    placed = (
        P("group", "slab", None),
        P(),
        P(None, None, "slab"),
        P(),
        P(),
        P("slab", None),
        P(),
        P(),
    )
    return jax.shard_map(
        body, mesh=mesh, in_specs=placed, out_specs=P("group", "slab", None), check_vma=False
    )
```

```python
import functools
import math

import jax
import jax.numpy as jnp
from jax import lax
from jax.sharding import PartitionSpec as P
from jax.experimental import pallas as pl
from jax.experimental.pallas import tpu as pltpu

REACH = 3


def shifted(block, axis, distance):
    devices = range(lax.axis_size(axis))
    route = [(i - distance, i) for i in devices if i - distance in devices]
    return lax.ppermute(block, axis, route)


def rotated(block, axis, distance):
    count = lax.axis_size(axis)
    route = [(i, (i + distance) % count) for i in range(count)]
    return lax.ppermute(block, axis, route)


def norm_rows(values, gain):
    centre = jnp.mean(values, axis=-1, keepdims=True)
    centred = values - centre
    spread = jnp.mean(centred * centred, axis=-1, keepdims=True)
    return centred * lax.rsqrt(spread + 1e-06) * gain


def block_terms(queries, key_rows, values, score_scale):
    scores = (
        jnp.einsum("qhd,khd->hqk", queries, key_rows, preferred_element_type=jnp.float32)
        * score_scale
    )
    weights = jnp.exp(scores).astype(jnp.bfloat16)
    numerator = jnp.einsum("hqk,khd->qhd", weights, values, preferred_element_type=jnp.float32)
    denominator = jnp.transpose(jnp.sum(weights, axis=2, dtype=jnp.float32))
    return (numerator, denominator)


def attention_kernel(q_ref, k_ref, v_ref, num_in, den_in, num_out, den_out, *, head_size, scale):
    queries = q_ref[...]
    keys = k_ref[...]
    values = v_ref[...]
    first = lax.broadcasted_iota(jnp.int32, (1, 2 * head_size), 1) < head_size
    parts = []
    for lanes in (first, jnp.logical_not(first)):
        head_keys = jnp.where(lanes, keys, jnp.zeros_like(keys))
        scores = lax.dot_general(
            queries, head_keys, (((1,), (1,)), ((), ())), preferred_element_type=jnp.float32
        )
        weights = jnp.exp(scores).astype(jnp.bfloat16)
        numerator = jnp.dot(weights, values, preferred_element_type=jnp.float32)
        denominator = jnp.sum(weights.astype(jnp.float32), axis=1, keepdims=True)
        parts.append((numerator, denominator))
    num_out[...] = num_in[...] + jnp.where(first, parts[0][0], parts[1][0])
    den_out[...] = den_in[...] + jnp.where(first, parts[0][1], parts[1][1])


def project_kernel(
    x_ref, w_ref, q_gain_ref, k_gain_ref, q_in, kv_in, q_ref, kv_ref, piece_ref, *, head_size, width, q_scale
):
    first = lax.broadcasted_iota(jnp.int32, (1, 2 * head_size), 1) < head_size

    def head_norm(values, gain):
        def head_mean(x):
            total_a = jnp.sum(jnp.where(first, x, 0.0), axis=1, keepdims=True)
            total_b = jnp.sum(jnp.where(first, 0.0, x), axis=1, keepdims=True)
            return jnp.where(first, total_a, total_b) / head_size

        centred = values - head_mean(values)
        spread = head_mean(centred * centred)
        return centred * lax.rsqrt(spread + 1e-06) * gain

    rows = x_ref[...]
    for part in range(3):
        projected = jnp.dot(
            rows, w_ref[part], preferred_element_type=jnp.float32
        )
        for pair in range(width // (2 * head_size)):
            lanes = slice(pair * 2 * head_size, (pair + 1) * 2 * head_size)
            if part == 0:
                rounded = head_norm(projected[:, lanes], q_gain_ref[...]).astype(q_ref.dtype)
                q_ref[:, lanes] = rounded * jnp.asarray(q_scale, q_ref.dtype)
            else:
                if part == 1:
                    block = head_norm(projected[:, lanes], k_gain_ref[...]).astype(kv_ref.dtype)
                else:
                    block = projected[:, lanes].astype(kv_ref.dtype)
                kv_ref[part - 1, :, lanes] = block
                piece_ref[part - 1, :, lanes] = block


def project_heads(rows, part_w, q_gain, k_gain, head_size, q_buf, kv_buf, row_start):
    assert math.log2(head_size) % 2 == 0
    row_count, full_width = rows.shape
    width = part_w.shape[2]
    tile = 256 if row_count % 256 == 0 else 128
    first_tile = row_start // tile
    pair_gain = lambda gain: jnp.tile(gain, 2).reshape(1, 2 * head_size)
    gain_spec = pl.BlockSpec((1, 2 * head_size), lambda i: (0, 0))
    q_spec = pl.BlockSpec((tile, width), lambda i: (i + first_tile, 0))
    kv_spec = pl.BlockSpec((2, tile, width), lambda i: (0, i + first_tile, 0))
    return pl.pallas_call(
        functools.partial(project_kernel, head_size=head_size, width=width, q_scale=head_size ** (-0.5)),
        grid=(row_count // tile,),
        in_specs=[
            pl.BlockSpec((tile, full_width), lambda i: (i, 0)),
            pl.BlockSpec((3, full_width, width), lambda i: (0, 0, 0)),
            gain_spec,
            gain_spec,
            q_spec,
            kv_spec,
        ],
        out_specs=[q_spec, kv_spec, pl.BlockSpec((2, tile, width), lambda i: (0, i, 0))],
        out_shape=[
            jax.ShapeDtypeStruct(q_buf.shape, jnp.bfloat16),
            jax.ShapeDtypeStruct(kv_buf.shape, jnp.bfloat16),
            jax.ShapeDtypeStruct((2, row_count, width), jnp.bfloat16),
        ],
        input_output_aliases={4: 0, 5: 1},
        cost_estimate=pl.CostEstimate(
            flops=2 * row_count * full_width * 3 * width,
            transcendentals=row_count * width,
            bytes_accessed=row_count * full_width * 2 + full_width * 6 * width + row_count * width * 6,
        ),
    )(rows, part_w, pair_gain(q_gain), pair_gain(k_gain), q_buf, kv_buf)


def attend_block(queries, held, numerator, denominator, row_start, row_count, head_size, scale):
    token_count, width = queries.shape
    key_count = held.shape[1]
    pair_width = 2 * head_size
    tile = min(math.gcd(row_start, row_count) if row_start else row_count, 1024)
    first_tile = row_start // tile
    row_spec = pl.BlockSpec((tile, pair_width), lambda i, j: (i + first_tile, j))
    key_spec = pl.BlockSpec((None, key_count, pair_width), lambda i, j: (0, 0, j))
    value_spec = pl.BlockSpec((None, key_count, pair_width), lambda i, j: (1, 0, j))
    flops = 2 * 2 * 2 * row_count * key_count * width
    return pl.pallas_call(
        functools.partial(attention_kernel, head_size=head_size, scale=scale),
        grid=(row_count // tile, width // pair_width),
        in_specs=[row_spec, key_spec, value_spec, row_spec, row_spec],
        out_specs=[row_spec, row_spec],
        out_shape=[jax.ShapeDtypeStruct((token_count, width), jnp.float32)] * 2,
        input_output_aliases={3: 0, 4: 1},
        compiler_params=pltpu.CompilerParams(dimension_semantics=("arbitrary", "arbitrary")),
        cost_estimate=pl.CostEstimate(
            flops=flops,
            transcendentals=row_count * key_count * (width // head_size),
            bytes_accessed=row_count * width * 18 + key_count * width * 4 * (row_count // tile),
        ),
    )(queries, held, held, numerator, denominator)


def body(tokens, norm_gain, w_qkv, q_gain, k_gain, w_out, covis_mask, capture_rank):
    full_width = tokens.shape[2]
    local_width = w_qkv.shape[2]
    head_size = q_gain.shape[0]
    heads_here = local_width // head_size
    score_scale = head_size ** (-0.5)
    slab_count = lax.axis_size("slab")
    my_group = lax.axis_index("group")
    group_count = lax.axis_size("group")
    normed = norm_rows(tokens[0].astype(jnp.float32), norm_gain).astype(jnp.bfloat16)
    piece_rows = normed.shape[0]
    part_w = jnp.transpose(w_qkv, (1, 0, 2))

    token_count = tokens.shape[1] * slab_count

    def project(rows, buffers, row_start):
        return project_heads(rows, part_w, q_gain, k_gain, head_size, *buffers, row_start)

    empty = (
        jnp.zeros((token_count, local_width), jnp.bfloat16),
        jnp.zeros((2, token_count, local_width), jnp.bfloat16),
    )
    own_q, own_pairs, own_piece = project(normed, empty, 0)

    def allowed_from(source):
        in_range = (source >= 0) & (source < group_count)
        clipped = jnp.clip(source, 0, group_count - 1)
        return (
            in_range
            & (covis_mask[my_group, clipped] == 1)
            & (capture_rank[clipped] <= capture_rank[my_group])
        )

    def routed(block, route):
        return lax.ppermute(block, "group", [(a, b) for a, b in route if 0 <= b < group_count])

    g_all = range(group_count)
    spot = my_group % 4
    on_chip = [(g, g ^ 1) for g in g_all]
    across_x = [(g, g ^ 2) for g in g_all]
    along_z_once = [(g, g + 3) if g % 2 == 1 else (g, g - 3) for g in g_all]
    mixed_relay = [
        (g, g ^ 2) if g % 4 in (1, 2) else ((g, g + 5) if g % 4 == 0 else (g, g - 5)) for g in g_all
    ]

    def round_one(buf, from_x):
        return [
            (my_group ^ 1, routed(buf, on_chip)),
            (my_group ^ 2, from_x),
            (jnp.where(spot % 2 == 0, my_group - 3, my_group + 3), routed(buf, along_z_once)),
        ]

    def round_two(first):
        from_x, from_z = first[1][1], first[2][1]
        outgoing = jnp.where((spot == 1) | (spot == 2), from_z, from_x)
        source = jnp.where(
            spot == 0,
            my_group - 1,
            jnp.where(spot == 1, my_group - 3, jnp.where(spot == 2, my_group + 3, my_group + 1)),
        )
        return [
            (my_group ^ 3, routed(from_x, on_chip)),
            (source, routed(outgoing, mixed_relay)),
        ]

    def round_three(second):
        return [(jnp.where(spot < 2, my_group - 2, my_group + 2), routed(second[1][1], on_chip))]

    early_x = routed(own_piece, across_x)
    queries, pairs = own_q, own_pairs
    w_pieces = [w_out]
    if slab_count > 1:
        gathered = [rotated(normed, "slab", k) for k in range(1, slab_count)]
        w_later = lax.optimization_barrier((w_out, gathered))[0]
        w_pieces = w_pieces + [rotated(w_later, "slab", -k) for k in range(1, slab_count)]
        gathered, early_x = lax.optimization_barrier((gathered, early_x))
        queries, pairs, rest_piece = project(jnp.concatenate(gathered, axis=0), (own_q, own_pairs), piece_rows)

    def add_terms(held, sums, row_start=0, row_count=None):
        row_count = token_count if row_count is None else row_count
        return tuple(
            attend_block(queries, held, sums[0], sums[1], row_start, row_count, head_size, score_scale)
        )

    def add_masked(arrived, sums, row_start=0, row_count=None):
        for source, held in arrived:
            sums = lax.cond(
                allowed_from(source),
                lambda: add_terms(held, sums, row_start, row_count),
                lambda: sums,
            )
        return sums

    zeros = jnp.zeros((token_count, local_width), jnp.float32)
    from_x = early_x
    if slab_count > 1:
        from_x = jnp.concatenate([early_x, routed(rest_piece, across_x)], axis=1)
    first = round_one(pairs, from_x)
    if slab_count > 1:
        sums = attend_block(own_q, own_piece, zeros, zeros, 0, piece_rows, head_size, score_scale)
        sums = add_terms(own_piece, sums, piece_rows, token_count - piece_rows)
        sums = add_terms(rest_piece, sums)
    else:
        sums = add_terms(pairs, (zeros, zeros))
    first, sums, w_pieces = lax.optimization_barrier((first, sums, w_pieces))
    second = round_two(first)
    sums = add_masked(first, sums)
    second, sums = lax.optimization_barrier((second, sums))
    last = round_three(second)
    sums = add_masked(second, sums)
    last, sums = lax.optimization_barrier((last, sums))

    att_pieces = [None] * slab_count
    for k in list(range(1, slab_count)) + [0]:
        row_start = k * piece_rows
        sums = add_masked(last, sums, row_start, piece_rows)
        rows = slice(row_start, row_start + piece_rows)
        attended = (sums[0][rows] / sums[1][rows]).astype(jnp.bfloat16)
        if k != 0:
            attended, last, sums = lax.optimization_barrier((attended, last, sums))
            attended = rotated(attended, "slab", -k)
        att_pieces[k] = attended
    mixed = jnp.dot(
        jnp.concatenate(att_pieces, axis=1),
        jnp.concatenate(w_pieces, axis=0),
        preferred_element_type=jnp.float32,
    )
    return mixed.astype(jnp.bfloat16)[None]


def solution(mesh):
    placed = (
        P("group", "slab", None),
        P(),
        P(None, None, "slab"),
        P(),
        P(),
        P("slab", None),
        P(),
        P(),
    )
    return jax.shard_map(
        body, mesh=mesh, in_specs=placed, out_specs=P("group", "slab", None), check_vma=False
    )
```

```python
import functools
import math

import jax
import jax.numpy as jnp
from jax import lax
from jax.sharding import PartitionSpec as P
from jax.experimental import pallas as pl
from jax.experimental.pallas import tpu as pltpu

REACH = 3


def shifted(block, axis, distance):
    devices = range(lax.axis_size(axis))
    route = [(i - distance, i) for i in devices if i - distance in devices]
    return lax.ppermute(block, axis, route)


def rotated(block, axis, distance):
    count = lax.axis_size(axis)
    route = [(i, (i + distance) % count) for i in range(count)]
    return lax.ppermute(block, axis, route)


def norm_rows(values, gain):
    centre = jnp.mean(values, axis=-1, keepdims=True)
    centred = values - centre
    spread = jnp.mean(centred * centred, axis=-1, keepdims=True)
    return centred * lax.rsqrt(spread + 1e-06) * gain


def block_terms(queries, key_rows, values, score_scale):
    scores = (
        jnp.einsum("qhd,khd->hqk", queries, key_rows, preferred_element_type=jnp.float32)
        * score_scale
    )
    weights = jnp.exp(scores).astype(jnp.bfloat16)
    numerator = jnp.einsum("hqk,khd->qhd", weights, values, preferred_element_type=jnp.float32)
    denominator = jnp.transpose(jnp.sum(weights, axis=2, dtype=jnp.float32))
    return (numerator, denominator)


def attention_kernel(q_ref, k_ref, v_ref, num_in, den_in, num_out, den_out, *, head_size, scale):
    queries = q_ref[...]
    keys = k_ref[...]
    values = v_ref[...]
    first = lax.broadcasted_iota(jnp.int32, (1, 2 * head_size), 1) < head_size
    parts = []
    for lanes in (first, jnp.logical_not(first)):
        head_keys = jnp.where(lanes, keys, jnp.zeros_like(keys))
        scores = lax.dot_general(
            queries, head_keys, (((1,), (1,)), ((), ())), preferred_element_type=jnp.float32
        )
        weights = jnp.exp(scores).astype(jnp.bfloat16)
        numerator = jnp.dot(weights, values, preferred_element_type=jnp.float32)
        denominator = jnp.sum(weights.astype(jnp.float32), axis=1, keepdims=True)
        parts.append((numerator, denominator))
    num_out[...] = num_in[...] + jnp.where(first, parts[0][0], parts[1][0])
    den_out[...] = den_in[...] + jnp.where(first, parts[0][1], parts[1][1])


def project_kernel(
    x_ref, w_ref, q_gain_ref, k_gain_ref, q_in, kv_in, q_ref, kv_ref, piece_ref, *, head_size, width, q_scale
):
    first = lax.broadcasted_iota(jnp.int32, (1, 2 * head_size), 1) < head_size

    def head_norm(values, gain):
        def head_mean(x):
            total_a = jnp.sum(jnp.where(first, x, 0.0), axis=1, keepdims=True)
            total_b = jnp.sum(jnp.where(first, 0.0, x), axis=1, keepdims=True)
            return jnp.where(first, total_a, total_b) / head_size

        centred = values - head_mean(values)
        spread = head_mean(centred * centred)
        return centred * lax.rsqrt(spread + 1e-06) * gain

    rows = x_ref[...]
    for part in range(3):
        projected = jnp.dot(
            rows, w_ref[part], preferred_element_type=jnp.float32
        )
        for pair in range(width // (2 * head_size)):
            lanes = slice(pair * 2 * head_size, (pair + 1) * 2 * head_size)
            if part == 0:
                rounded = head_norm(projected[:, lanes], q_gain_ref[...]).astype(q_ref.dtype)
                q_ref[:, lanes] = rounded * jnp.asarray(q_scale, q_ref.dtype)
            else:
                if part == 1:
                    block = head_norm(projected[:, lanes], k_gain_ref[...]).astype(kv_ref.dtype)
                else:
                    block = projected[:, lanes].astype(kv_ref.dtype)
                kv_ref[part - 1, :, lanes] = block
                piece_ref[part - 1, :, lanes] = block


def project_heads(rows, part_w, q_gain, k_gain, head_size, q_buf, kv_buf, row_start):
    assert math.log2(head_size) % 2 == 0
    row_count, full_width = rows.shape
    width = part_w.shape[2]
    tile = 256 if row_count % 256 == 0 else 128
    first_tile = row_start // tile
    pair_gain = lambda gain: jnp.tile(gain, 2).reshape(1, 2 * head_size)
    gain_spec = pl.BlockSpec((1, 2 * head_size), lambda i: (0, 0))
    q_spec = pl.BlockSpec((tile, width), lambda i: (i + first_tile, 0))
    kv_spec = pl.BlockSpec((2, tile, width), lambda i: (0, i + first_tile, 0))
    return pl.pallas_call(
        functools.partial(project_kernel, head_size=head_size, width=width, q_scale=head_size ** (-0.5)),
        grid=(row_count // tile,),
        in_specs=[
            pl.BlockSpec((tile, full_width), lambda i: (i, 0)),
            pl.BlockSpec((3, full_width, width), lambda i: (0, 0, 0)),
            gain_spec,
            gain_spec,
            q_spec,
            kv_spec,
        ],
        out_specs=[q_spec, kv_spec, pl.BlockSpec((2, tile, width), lambda i: (0, i, 0))],
        out_shape=[
            jax.ShapeDtypeStruct(q_buf.shape, jnp.bfloat16),
            jax.ShapeDtypeStruct(kv_buf.shape, jnp.bfloat16),
            jax.ShapeDtypeStruct((2, row_count, width), jnp.bfloat16),
        ],
        input_output_aliases={4: 0, 5: 1},
        cost_estimate=pl.CostEstimate(
            flops=2 * row_count * full_width * 3 * width,
            transcendentals=row_count * width,
            bytes_accessed=row_count * full_width * 2 + full_width * 6 * width + row_count * width * 6,
        ),
    )(rows, part_w, pair_gain(q_gain), pair_gain(k_gain), q_buf, kv_buf)


def attend_block(queries, held, numerator, denominator, row_start, row_count, head_size, scale):
    token_count, width = queries.shape
    key_count = held.shape[1]
    pair_width = 2 * head_size
    tile = min(math.gcd(row_start, row_count) if row_start else row_count, 1024)
    first_tile = row_start // tile
    row_spec = pl.BlockSpec((tile, pair_width), lambda i, j: (i + first_tile, j))
    key_spec = pl.BlockSpec((None, key_count, pair_width), lambda i, j: (0, 0, j))
    value_spec = pl.BlockSpec((None, key_count, pair_width), lambda i, j: (1, 0, j))
    flops = 2 * 2 * 2 * row_count * key_count * width
    return pl.pallas_call(
        functools.partial(attention_kernel, head_size=head_size, scale=scale),
        grid=(row_count // tile, width // pair_width),
        in_specs=[row_spec, key_spec, value_spec, row_spec, row_spec],
        out_specs=[row_spec, row_spec],
        out_shape=[jax.ShapeDtypeStruct((token_count, width), jnp.float32)] * 2,
        input_output_aliases={3: 0, 4: 1},
        compiler_params=pltpu.CompilerParams(dimension_semantics=("arbitrary", "arbitrary")),
        cost_estimate=pl.CostEstimate(
            flops=flops,
            transcendentals=row_count * key_count * (width // head_size),
            bytes_accessed=row_count * width * 18 + key_count * width * 4 * (row_count // tile),
        ),
    )(queries, held, held, numerator, denominator)


def body(tokens, norm_gain, w_qkv, q_gain, k_gain, w_out, covis_mask, capture_rank):
    full_width = tokens.shape[2]
    local_width = w_qkv.shape[2]
    head_size = q_gain.shape[0]
    heads_here = local_width // head_size
    score_scale = head_size ** (-0.5)
    slab_count = lax.axis_size("slab")
    my_group = lax.axis_index("group")
    group_count = lax.axis_size("group")
    normed = norm_rows(tokens[0].astype(jnp.float32), norm_gain).astype(jnp.bfloat16)
    piece_rows = normed.shape[0]
    part_w = jnp.transpose(w_qkv, (1, 0, 2))

    token_count = tokens.shape[1] * slab_count

    def project(rows, buffers, row_start):
        return project_heads(rows, part_w, q_gain, k_gain, head_size, *buffers, row_start)

    empty = (
        jnp.zeros((token_count, local_width), jnp.bfloat16),
        jnp.zeros((2, token_count, local_width), jnp.bfloat16),
    )
    own_q, own_pairs, own_piece = project(normed, empty, 0)

    def allowed_from(source):
        in_range = (source >= 0) & (source < group_count)
        clipped = jnp.clip(source, 0, group_count - 1)
        return (
            in_range
            & (covis_mask[my_group, clipped] == 1)
            & (capture_rank[clipped] <= capture_rank[my_group])
        )

    def routed(block, route):
        return lax.ppermute(block, "group", [(a, b) for a, b in route if 0 <= b < group_count])

    g_all = range(group_count)
    spot = my_group % 4
    on_chip = [(g, g ^ 1) for g in g_all]
    across_x = [(g, g ^ 2) for g in g_all]
    along_z_once = [(g, g + 3) if g % 2 == 1 else (g, g - 3) for g in g_all]
    mixed_relay = [
        (g, g ^ 2) if g % 4 in (1, 2) else ((g, g + 5) if g % 4 == 0 else (g, g - 5)) for g in g_all
    ]

    def round_one(buf, from_x):
        return [
            (my_group ^ 1, routed(buf, on_chip)),
            (my_group ^ 2, from_x),
            (jnp.where(spot % 2 == 0, my_group - 3, my_group + 3), routed(buf, along_z_once)),
        ]

    def round_two(first):
        from_x, from_z = first[1][1], first[2][1]
        outgoing = jnp.where((spot == 1) | (spot == 2), from_z, from_x)
        source = jnp.where(
            spot == 0,
            my_group - 1,
            jnp.where(spot == 1, my_group - 3, jnp.where(spot == 2, my_group + 3, my_group + 1)),
        )
        return [
            (my_group ^ 3, routed(from_x, on_chip)),
            (source, routed(outgoing, mixed_relay)),
        ]

    def round_three(second):
        return [(jnp.where(spot < 2, my_group - 2, my_group + 2), routed(second[1][1], on_chip))]

    early_x = routed(own_piece, across_x)
    queries, pairs = own_q, own_pairs
    w_pieces = [w_out]
    if slab_count > 1:
        gathered = [rotated(normed, "slab", k) for k in range(1, slab_count)]
        w_later = lax.optimization_barrier((w_out, gathered))[0]
        w_pieces = w_pieces + [rotated(w_later, "slab", -k) for k in range(1, slab_count)]
        gathered, early_x = lax.optimization_barrier((gathered, early_x))
        queries, pairs, rest_piece = project(jnp.concatenate(gathered, axis=0), (own_q, own_pairs), piece_rows)

    def add_terms(held, sums, row_start=0, row_count=None):
        row_count = token_count if row_count is None else row_count
        return tuple(
            attend_block(queries, held, sums[0], sums[1], row_start, row_count, head_size, score_scale)
        )

    def add_masked(arrived, sums, row_start=0, row_count=None):
        for source, held in arrived:
            sums = lax.cond(
                allowed_from(source),
                lambda: add_terms(held, sums, row_start, row_count),
                lambda: sums,
            )
        return sums

    zeros = jnp.zeros((token_count, local_width), jnp.float32)
    from_x = early_x
    if slab_count > 1:
        from_x = jnp.concatenate([early_x, routed(rest_piece, across_x)], axis=1)
    first = round_one(pairs, from_x)
    if slab_count > 1:
        sums = attend_block(own_q, own_piece, zeros, zeros, 0, piece_rows, head_size, score_scale)
        sums = add_terms(own_piece, sums, piece_rows, token_count - piece_rows)
        sums = add_terms(rest_piece, sums)
    else:
        sums = add_terms(pairs, (zeros, zeros))
    first, sums, w_pieces = lax.optimization_barrier((first, sums, w_pieces))
    second = round_two(first)
    sums = add_masked(first, sums)
    second, sums = lax.optimization_barrier((second, sums))
    last = round_three(second)
    sums = add_masked(second, sums)
    last, sums = lax.optimization_barrier((last, sums))

    att_pieces = [None] * slab_count
    for k in list(range(1, slab_count)) + [0]:
        row_start = k * piece_rows
        sums = add_masked(last, sums, row_start, piece_rows)
        rows = slice(row_start, row_start + piece_rows)
        attended = (sums[0][rows] / sums[1][rows]).astype(jnp.bfloat16)
        if k != 0:
            attended, last, sums = lax.optimization_barrier((attended, last, sums))
            attended = rotated(attended, "slab", -k)
        att_pieces[k] = attended
    mixed = jnp.dot(att_pieces[0], w_pieces[0], preferred_element_type=jnp.float32)
    if slab_count > 1:
        arrived, mixed = lax.optimization_barrier((att_pieces[1:], mixed))
        mixed = mixed + jnp.dot(
            jnp.concatenate(arrived, axis=1),
            jnp.concatenate(w_pieces[1:], axis=0),
            preferred_element_type=jnp.float32,
        )
    return mixed.astype(jnp.bfloat16)[None]


def solution(mesh):
    placed = (
        P("group", "slab", None),
        P(),
        P(None, None, "slab"),
        P(),
        P(),
        P("slab", None),
        P(),
        P(),
    )
    return jax.shard_map(
        body, mesh=mesh, in_specs=placed, out_specs=P("group", "slab", None), check_vma=False
    )
```
